32 devices in a mesh: groups: 2 (over x), chan: 16 (over z, y, core), freq: 1.
Axes of the slice: x: 2, y: 2, z: 4, core: 2. Of those that a mesh axis runs over, the one named last changes fastest.
Arguments:
- raw: bfloat16 [256, 16, 12000], P(('groups', 'chan'), 'freq'), parts along dimension 0, may hold values from -100 to 100, as said below
- lengths: int32 [256, 16], P(('groups', 'chan'), 'freq'), parts along dimension 0, may hold values from 6000 to 12000
- quality: int32 [256], P('groups'), parts along dimension 0, may hold values 0 or 1
- assignment: int32 [256], P('groups'), parts along dimension 0, may hold values from 0 to 127, as said below
Outputs:
- cross: bfloat16 [512, 256, 2, 128], P('freq', ('groups', 'chan')), parts along dimension 1
The draws below stay inside these ranges and needn't reach their ends.
There are 2 independent parts, one for each index of `groups`. The reference program is written for one: setup_inputs(seed, part) draws one part's arguments, and reference() takes and returns one part's arrays. A program takes and returns all parts, laid end to end along the dimension named above; each array names one. Nothing has to cross between parts.
Inputs may be any that keep to these rules, and one draw needn't show every extreme that they name: `raw`: records are clipped to this range. `assignment`: A permutation. The 8 channels of one file block (consecutive entries) land at most 1 in any one block of 8 consecutive positions, and some pair of blocks reaches 1.
All inputs are finite; a program needn't handle non-finite values.
Results may differ from the reference program's by a relative error of at most 0.012.
The reference program's roundings to bfloat16 on the way count: a program that leaves them out, or rounds other values in their place, can miss the bound.
Values may be sent and summed in bfloat16 or wider, within the bound.
No kernel may reach another device: no remote copies, remote signals or barrier semaphores. Data moves between devices by JAX's collectives and lax.ppermute only.
A program may use at most 128 MiB of HBM per device.

```python
import math
import jax
import jax.numpy as jnp
from jax import lax

CH_BLK = 8
W = 16
WIN = 12000
NB = 512
K0 = 6
SUB = 32
CH = 128
CAP = 1


def draw_raw(key, part):
    keys = jax.random.split(jax.random.fold_in(key, 11), 5)
    samples = jnp.arange(WIN, dtype=jnp.int32)
    spread = math.log(10.0)
    values = jax.random.truncated_normal(keys[1], -4.0, 4.0, (CH, W, WIN), jnp.float32)
    scales = jnp.exp(jax.random.uniform(keys[0], (CH, 1, 1), jnp.float32) * spread)
    tone_bins = jax.random.randint(keys[2], (CH, 6), K0, K0 + NB)
    tone_sizes = jnp.exp(jax.random.uniform(keys[3], (CH, 6), jnp.float32, math.log(0.5), math.log(5.0)))
    phases = jax.random.uniform(keys[4], (CH, W, 6), jnp.float32, 0.0, 2.0 * math.pi)
    for number in range(6):
        residue = tone_bins[:, number, None, None] * samples[None, None, :] % WIN
        angles = residue.astype(jnp.float32) * (2.0 * math.pi / WIN) + phases[:, :, number, None]
        values = values + tone_sizes[:, number, None, None] * jnp.cos(angles)
    return jnp.clip(scales * values, -100.0, 100.0).astype(jnp.bfloat16)


def draw_assignment(key, part):
    keys = jax.random.split(jax.random.fold_in(key, 23), 4)
    groups_count = CH // CH_BLK
    offsets = jax.random.permutation(keys[0], groups_count * CAP)[:CH_BLK] // CAP
    source_order = jax.random.permutation(keys[1], groups_count)
    target_order = jax.random.permutation(keys[2], groups_count)
    arrival = jax.vmap(lambda subkey: jax.random.permutation(subkey, CH_BLK))(jax.random.split(keys[3], groups_count))
    targets = target_order[(source_order[:, None] + offsets[None, :]) % groups_count]
    row_numbers = jnp.broadcast_to(jnp.arange(CH_BLK, dtype=jnp.int32)[None, :], targets.shape)
    return (targets * CH_BLK + arrival[targets, row_numbers]).reshape(CH).astype(jnp.int32)


def place_ends(result, own_key, low, top_value):
    longest = result.shape.index(max(result.shape))
    spots = []
    for shift in (0, 1):
        where = [jax.random.randint(jax.random.fold_in(own_key, axis), (), 0, length) for axis, length in enumerate(result.shape)]
        where[longest] = (where[longest] + shift) % result.shape[longest]
        spots.append(tuple(where))
    return result.at[spots[0]].set(low).at[spots[1]].set(top_value)


def setup_inputs(seed: int = 0, part: int = 0) -> dict:
    splits = jax.random.split(jax.random.key(seed), 5)
    part_keys = jax.random.split(jax.random.fold_in(splits[4], part), 5)
    return {
        "raw": draw_raw(jax.random.fold_in(jax.random.fold_in(splits[4], part), 71), part),
        "lengths": place_ends(jax.random.randint(part_keys[1], (CH, W), WIN // 2, WIN + 1), jax.random.fold_in(part_keys[1], 1), WIN // 2, WIN).astype(jnp.int32),
        "quality": place_ends((jax.random.randint(part_keys[2], (CH,), 0, 8) < 7).astype(jnp.int32), jax.random.fold_in(part_keys[2], 1), 0, 1),
        "assignment": draw_assignment(jax.random.fold_in(jax.random.fold_in(splits[4], part), 71), part),
    }


def dft_table(first_sample, sample_count):
    samples = first_sample + jnp.arange(sample_count, dtype=jnp.int32)
    bin_index = K0 + jnp.arange(NB, dtype=jnp.int32)
    residue = samples[:, None] * bin_index[None, :] % WIN
    angles = residue.astype(jnp.float32) * (2.0 * math.pi / WIN)
    return jnp.concatenate([jnp.cos(angles), -jnp.sin(angles)], axis=1).astype(jnp.bfloat16)

def prepare(raw_block, valid_lengths):
    positions = jnp.arange(WIN, dtype=jnp.int32)
    inside = positions[None, None, :] < valid_lengths[:, :, None]
    values = raw_block.astype(jnp.float32)
    kept = jnp.where(inside, values, 0.0)
    average = lax.optimization_barrier(jnp.sum(kept, axis=-1)) / valid_lengths.astype(jnp.float32)
    taper = 0.5 - 0.5 * jnp.cos(positions.astype(jnp.float32) * (2.0 * math.pi / WIN))
    return jnp.where(inside, (values - average[:, :, None]) * taper[None, None, :], 0.0).astype(jnp.bfloat16)

def whiten(spectra):
    row_count = spectra.shape[0]
    grouped = spectra.reshape(row_count, 2, NB // SUB, SUB)
    power = lax.optimization_barrier(jnp.sum(grouped * grouped, axis=(1, 3))) / SUB
    factor = lax.rsqrt(power + 1e-06)
    return (grouped * factor[:, None, :, None]).reshape(row_count, 2, NB).astype(jnp.bfloat16)

def reference(raw, lengths, quality, assignment):
    shaped = prepare(raw, lengths)
    spectra = jnp.dot(shaped.reshape(CH * W, WIN), dft_table(0, WIN), preferred_element_type=jnp.float32)
    whitened = whiten(spectra).reshape(CH, W, 2, NB)
    whitened = whitened * quality.astype(jnp.bfloat16)[:, None, None, None]
    ordered = jnp.zeros_like(whitened).at[assignment].set(whitened)
    turned = jnp.stack([-ordered[:, :, 1], ordered[:, :, 0]], axis=2)
    left_all = ordered.transpose(3, 0, 2, 1).reshape(NB, CH, 2 * W).astype(jnp.float32)
    right_plain = ordered.transpose(3, 2, 1, 0).reshape(NB, 2 * W, CH).astype(jnp.float32)
    right_turned = turned.transpose(3, 2, 1, 0).reshape(NB, 2 * W, CH).astype(jnp.float32)
    left_blocks = left_all.reshape(NB, CH // CH_BLK, CH_BLK, 2 * W).transpose(1, 0, 2, 3)

    def one_block(left):
        real_part = jnp.einsum('bik,bkj->bij', left, right_plain, precision=lax.Precision.HIGHEST)
        imag_part = jnp.einsum('bik,bkj->bij', left, right_turned, precision=lax.Precision.HIGHEST)
        return (jnp.stack([real_part, imag_part], axis=2) / W).astype(jnp.bfloat16)
    blocks = lax.map(one_block, left_blocks)
    return blocks.transpose(1, 0, 2, 3, 4).reshape(NB, CH, 2, CH)
```

```python
import math

import jax
import jax.numpy as jnp
from jax import lax
from jax.sharding import PartitionSpec as P

WIN = 12000
NB = 512
K0 = 6
SUB = 32
SPLIT = 100


def small_table(sample_values):
    bin_index = K0 + jnp.arange(NB, dtype=jnp.int32)
    residue = sample_values[:, None] * bin_index[None, :] % WIN
    angles = residue.astype(jnp.float32) * (2.0 * math.pi / WIN)
    return jnp.cos(angles), jnp.sin(angles)


def dft_table():
    high = jnp.arange(WIN // SPLIT, dtype=jnp.int32) * SPLIT
    low = jnp.arange(SPLIT, dtype=jnp.int32)
    cos_high, sin_high = small_table(high)
    cos_low, sin_low = small_table(low)
    cos_all = cos_high[:, None, :] * cos_low[None, :, :] - sin_high[:, None, :] * sin_low[None, :, :]
    sin_all = sin_high[:, None, :] * cos_low[None, :, :] + cos_high[:, None, :] * sin_low[None, :, :]
    table = jnp.concatenate([cos_all, -sin_all], axis=2).astype(jnp.bfloat16)
    return table.reshape(WIN, 2 * NB)


def prepare(raw_block, valid_lengths):
    positions = jnp.arange(WIN, dtype=jnp.int32)
    inside = positions[None, None, :] < valid_lengths[:, :, None]
    values = raw_block.astype(jnp.float32)
    kept = jnp.where(inside, values, 0.0)
    average = jnp.sum(kept, axis=-1) / valid_lengths.astype(jnp.float32)
    taper = 0.5 - 0.5 * jnp.cos(positions.astype(jnp.float32) * (2.0 * math.pi / WIN))
    return jnp.where(inside, (values - average[:, :, None]) * taper[None, None, :], 0.0).astype(
        jnp.bfloat16
    )


def whiten(spectra):
    row_count = spectra.shape[0]
    grouped = spectra.reshape(row_count, 2, NB // SUB, SUB)
    power = jnp.sum(grouped * grouped, axis=(1, 3)) / SUB
    factor = lax.rsqrt(power + 1e-06)
    return (grouped * factor[:, None, :, None]).reshape(row_count, 2, NB).astype(jnp.bfloat16)


def body(raw, lengths, quality, assignment):
    my_index = lax.axis_index("chan")
    block_rows, window_count, sample_count = raw.shape
    total_channels = assignment.shape[0]
    shaped = prepare(raw, lengths)
    spectra = jnp.dot(
        shaped.reshape(block_rows * window_count, sample_count),
        dft_table(),
        preferred_element_type=jnp.float32,
    )
    whitened = whiten(spectra).reshape(block_rows, window_count, 2, NB)
    my_quality = lax.dynamic_slice_in_dim(quality, my_index * block_rows, block_rows)
    whitened = whitened * my_quality.astype(jnp.bfloat16)[:, None, None, None]
    panel = lax.all_to_all(whitened, "freq", split_axis=3, concat_axis=1, tiled=True)
    all_windows = panel.shape[1]
    bins_here = panel.shape[3]
    gathered = lax.all_gather(panel, "chan", axis=0, tiled=True)
    inverse = (
        jnp.zeros((total_channels,), jnp.int32)
        .at[assignment]
        .set(jnp.arange(total_channels, dtype=jnp.int32))
    )
    ordered = jnp.take(gathered, inverse, axis=0)
    mine = lax.dynamic_slice_in_dim(inverse, my_index * block_rows, block_rows)
    left = jnp.take(gathered, mine, axis=0)
    left_re = left[:, :, 0, :]
    left_im = left[:, :, 1, :]
    plain = jnp.stack([left_re, left_im], axis=1)
    turned = jnp.stack([left_im, -left_re], axis=1)
    left_rows = jnp.stack([plain, turned], axis=1)
    left_rows = left_rows.transpose(4, 0, 1, 2, 3).reshape(bins_here, block_rows * 2, 2 * all_windows)
    right = ordered.transpose(3, 2, 1, 0).reshape(bins_here, 2 * all_windows, total_channels)
    out = jnp.einsum("bik,bkj->bij", left_rows, right, preferred_element_type=jnp.float32)
    return (out / all_windows).astype(jnp.bfloat16).reshape(bins_here, block_rows, 2, total_channels)


def solution(mesh):
    return jax.shard_map(
        body,
        mesh=mesh,
        in_specs=(
            P(("groups", "chan"), "freq", None),
            P(("groups", "chan"), "freq"),
            P("groups"),
            P("groups"),
        ),
        out_specs=P("freq", ("groups", "chan"), None, None),
        check_vma=False,
    )
```

```python
import math

import jax
import jax.numpy as jnp
from jax import lax
from jax.experimental import pallas as pl
from jax.experimental.pallas import tpu as pltpu
from jax.sharding import PartitionSpec as P

WIN = 12000
NB = 512
K0 = 6
SUB = 32
LANE = 128
PADDED = 12288
TILES_PER_STEP = 8


def small_table(sample_values):
    bin_index = K0 + jnp.arange(NB, dtype=jnp.int32)
    residue = sample_values[:, None] * bin_index[None, :] % WIN
    angles = residue.astype(jnp.float32) * (2.0 * math.pi / WIN)
    return jnp.cos(angles), -jnp.sin(angles)


def dft_kernel(x_ref, cos_high_ref, sin_high_ref, cos_low_ref, sin_low_ref, out_ref):
    step = pl.program_id(0)

    @pl.when(step == 0)
    def _():
        out_ref[...] = jnp.zeros_like(out_ref)

    cos_low = cos_low_ref[...]
    sin_low = sin_low_ref[...]
    real_total = out_ref[:, :NB]
    imag_total = out_ref[:, NB:]
    for tile in range(TILES_PER_STEP):
        row = step * TILES_PER_STEP + tile
        cos_high = cos_high_ref[pl.ds(row, 1), :]
        sin_high = sin_high_ref[pl.ds(row, 1), :]
        cos_part = (cos_high * cos_low - sin_high * sin_low).astype(jnp.bfloat16)
        sin_part = (sin_high * cos_low + cos_high * sin_low).astype(jnp.bfloat16)
        samples = x_ref[:, tile * LANE:(tile + 1) * LANE]
        real_total = real_total + jnp.dot(samples, cos_part, preferred_element_type=jnp.float32)
        imag_total = imag_total + jnp.dot(samples, sin_part, preferred_element_type=jnp.float32)
    out_ref[:, :NB] = real_total
    out_ref[:, NB:] = imag_total


def spectra_of(shaped_rows):
    row_count = shaped_rows.shape[0]
    high_count = PADDED // LANE
    cos_high, sin_high = small_table(jnp.arange(high_count, dtype=jnp.int32) * LANE)
    cos_low, sin_low = small_table(jnp.arange(LANE, dtype=jnp.int32))
    block = TILES_PER_STEP * LANE
    steps = PADDED // block
    full = lambda shape: pl.BlockSpec(shape, lambda s: (0, 0))
    return pl.pallas_call(
        dft_kernel,
        out_shape=jax.ShapeDtypeStruct((row_count, 2 * NB), jnp.float32),
        grid=(steps,),
        in_specs=[
            pl.BlockSpec((row_count, block), lambda s: (0, s)),
            full((high_count, NB)),
            full((high_count, NB)),
            full((LANE, NB)),
            full((LANE, NB)),
        ],
        out_specs=full((row_count, 2 * NB)),
        compiler_params=pltpu.CompilerParams(dimension_semantics=("arbitrary",)),
        cost_estimate=pl.CostEstimate(
            flops=2 * row_count * PADDED * 2 * NB,
            transcendentals=0,
            bytes_accessed=row_count * PADDED * 2 + row_count * 2 * NB * 4,
        ),
    )(shaped_rows, cos_high, sin_high, cos_low, sin_low)


def prepare(raw_block, valid_lengths):
    positions = jnp.arange(PADDED, dtype=jnp.int32)
    inside = positions[None, None, :] < valid_lengths[:, :, None]
    pad = ((0, 0), (0, 0), (0, PADDED - raw_block.shape[2]))
    values = jnp.pad(raw_block, pad).astype(jnp.float32)
    kept = jnp.where(inside, values, 0.0)
    average = jnp.sum(kept, axis=-1) / valid_lengths.astype(jnp.float32)
    taper = 0.5 - 0.5 * jnp.cos(positions.astype(jnp.float32) * (2.0 * math.pi / WIN))
    return jnp.where(inside, (values - average[:, :, None]) * taper[None, None, :], 0.0).astype(
        jnp.bfloat16
    )


def whiten(spectra):
    row_count = spectra.shape[0]
    grouped = spectra.reshape(row_count, 2, NB // SUB, SUB)
    power = jnp.sum(grouped * grouped, axis=(1, 3)) / SUB
    factor = lax.rsqrt(power + 1e-06)
    return (grouped * factor[:, None, :, None]).reshape(row_count, 2, NB).astype(jnp.bfloat16)


def body(raw, lengths, quality, assignment):
    my_index = lax.axis_index("chan")
    block_rows, window_count, sample_count = raw.shape
    total_channels = assignment.shape[0]
    shaped = prepare(raw, lengths)
    spectra = spectra_of(shaped.reshape(block_rows * window_count, PADDED))
    whitened = whiten(spectra).reshape(block_rows, window_count, 2, NB)
    my_quality = lax.dynamic_slice_in_dim(quality, my_index * block_rows, block_rows)
    whitened = whitened * my_quality.astype(jnp.bfloat16)[:, None, None, None]
    panel = lax.all_to_all(whitened, "freq", split_axis=3, concat_axis=1, tiled=True)
    all_windows = panel.shape[1]
    bins_here = panel.shape[3]
    gathered = lax.all_gather(panel, "chan", axis=0, tiled=True)
    inverse = (
        jnp.zeros((total_channels,), jnp.int32)
        .at[assignment]
        .set(jnp.arange(total_channels, dtype=jnp.int32))
    )
    ordered = jnp.take(gathered, inverse, axis=0)
    mine = lax.dynamic_slice_in_dim(inverse, my_index * block_rows, block_rows)
    left = jnp.take(gathered, mine, axis=0)
    left_re = left[:, :, 0, :]
    left_im = left[:, :, 1, :]
    plain = jnp.stack([left_re, left_im], axis=1)
    turned = jnp.stack([left_im, -left_re], axis=1)
    left_rows = jnp.stack([plain, turned], axis=1)
    left_rows = left_rows.transpose(4, 0, 1, 2, 3).reshape(bins_here, block_rows * 2, 2 * all_windows)
    right = ordered.transpose(3, 2, 1, 0).reshape(bins_here, 2 * all_windows, total_channels)
    out = jnp.einsum("bik,bkj->bij", left_rows, right, preferred_element_type=jnp.float32)
    return (out / all_windows).astype(jnp.bfloat16).reshape(bins_here, block_rows, 2, total_channels)


def solution(mesh):
    return jax.shard_map(
        body,
        mesh=mesh,
        in_specs=(
            P(("groups", "chan"), "freq", None),
            P(("groups", "chan"), "freq"),
            P("groups"),
            P("groups"),
        ),
        out_specs=P("freq", ("groups", "chan"), None, None),
        check_vma=False,
    )
```

```python
import math

import numpy as np

import jax
import jax.numpy as jnp
from jax import lax
from jax.experimental import pallas as pl
from jax.experimental.pallas import tpu as pltpu
from jax.sharding import PartitionSpec as P

WIN = 12000
NB = 512
K0 = 6
SUB = 32
LANE = 128
PADDED = 12288
TILES_PER_STEP = 8


def small_table(sample_values):
    bin_index = K0 + np.arange(NB, dtype=np.int64)
    residue = sample_values[:, None] * bin_index[None, :] % WIN
    angles = residue.astype(np.float64) * (2.0 * math.pi / WIN)
    return np.cos(angles).astype(np.float32), (-np.sin(angles)).astype(np.float32)


def constant_tables():
    high_count = PADDED // LANE
    cos_high, sin_high = small_table(np.arange(high_count, dtype=np.int64) * LANE)
    cos_low, sin_low = small_table(np.arange(LANE, dtype=np.int64))
    positions = np.arange(PADDED, dtype=np.float64)
    taper = (0.5 - 0.5 * np.cos(positions * (2.0 * math.pi / WIN))).astype(np.float32)
    groups = (np.arange(NB)[:, None] // SUB == np.arange(NB // SUB)[None, :]).astype(np.float32)
    return cos_high, sin_high, cos_low, sin_low, taper.reshape(1, PADDED), groups


def dft_kernel(
    raw_ref, length_ref, quality_ref, taper_ref, cos_high_ref, sin_high_ref, cos_low_ref,
    sin_low_ref, groups_ref, out_ref, total_ref, mean_ref,
):
    phase = pl.program_id(0)
    step = pl.program_id(1)
    block = TILES_PER_STEP * LANE
    lengths = length_ref[...]

    @pl.when(jnp.logical_and(phase == 0, step == 0))
    def _():
        mean_ref[...] = jnp.zeros_like(mean_ref)
        total_ref[...] = jnp.zeros_like(total_ref)

    @pl.when(phase == 0)
    def _():
        positions = step * block + lax.broadcasted_iota(jnp.int32, raw_ref.shape, 1)
        inside = positions < lengths
        kept = jnp.where(inside, raw_ref[...].astype(jnp.float32), 0.0)
        mean_ref[...] += jnp.sum(kept, axis=1, keepdims=True)

    @pl.when(phase == 1)
    def _():
        average = mean_ref[...] / lengths.astype(jnp.float32)
        cos_low = cos_low_ref[...]
        sin_low = sin_low_ref[...]
        real_total = total_ref[:, :NB]
        imag_total = total_ref[:, NB:]
        for tile in range(TILES_PER_STEP):
            row = step * TILES_PER_STEP + tile
            cos_high = cos_high_ref[pl.ds(row, 1), :]
            sin_high = sin_high_ref[pl.ds(row, 1), :]
            cos_part = (cos_high * cos_low - sin_high * sin_low).astype(jnp.bfloat16)
            sin_part = (sin_high * cos_low + cos_high * sin_low).astype(jnp.bfloat16)
            values = raw_ref[:, tile * LANE:(tile + 1) * LANE].astype(jnp.float32)
            positions = row * LANE + lax.broadcasted_iota(jnp.int32, values.shape, 1)
            taper = taper_ref[:, pl.ds(pl.multiple_of(row * LANE, LANE), LANE)]
            samples = jnp.where(
                positions < lengths, (values - average) * taper, 0.0
            ).astype(jnp.bfloat16)
            real_total = real_total + jnp.dot(samples, cos_part, preferred_element_type=jnp.float32)
            imag_total = imag_total + jnp.dot(samples, sin_part, preferred_element_type=jnp.float32)
        total_ref[:, :NB] = real_total
        total_ref[:, NB:] = imag_total

        @pl.when(step == pl.num_programs(1) - 1)
        def _():
            groups = groups_ref[...]
            power = jnp.dot(
                real_total * real_total + imag_total * imag_total,
                groups,
                precision=lax.Precision.HIGHEST,
                preferred_element_type=jnp.float32,
            ) / SUB
            factor = lax.rsqrt(power + 1e-06)
            spread = lax.dot_general(
                factor, groups, (((1,), (1,)), ((), ())),
                precision=lax.Precision.HIGHEST,
                preferred_element_type=jnp.float32,
            )
            good = quality_ref[...] != 0
            real_out = (real_total * spread).astype(jnp.bfloat16)
            imag_out = (imag_total * spread).astype(jnp.bfloat16)
            zero = jnp.zeros_like(real_out)
            out_ref[:, :NB] = jnp.where(good, real_out, zero)
            out_ref[:, NB:] = jnp.where(good, imag_out, zero)


def whitened_of(raw_rows, length_rows, quality_rows):
    row_count = raw_rows.shape[0]
    tables = [jnp.asarray(t) for t in constant_tables()]
    block = TILES_PER_STEP * LANE
    steps = PADDED // block
    full = lambda shape: pl.BlockSpec(shape, lambda p, s: (0, 0))
    return pl.pallas_call(
        dft_kernel,
        out_shape=jax.ShapeDtypeStruct((row_count, 2 * NB), jnp.bfloat16),
        grid=(2, steps),
        in_specs=[
            pl.BlockSpec((row_count, block), lambda p, s: (0, s)),
            full((row_count, 1)),
            full((row_count, 1)),
            full((1, PADDED)),
            full(tables[1].shape),
            full(tables[1].shape),
            full(tables[2].shape),
            full(tables[2].shape),
            full(tables[5].shape),
        ],
        out_specs=full((row_count, 2 * NB)),
        scratch_shapes=[
            pltpu.VMEM((row_count, 2 * NB), jnp.float32),
            pltpu.VMEM((row_count, 1), jnp.float32),
        ],
        compiler_params=pltpu.CompilerParams(dimension_semantics=("arbitrary", "arbitrary")),
        cost_estimate=pl.CostEstimate(
            flops=2 * row_count * PADDED * 2 * NB,
            transcendentals=0,
            bytes_accessed=2 * row_count * WIN * 2 + row_count * 2 * NB * 2,
        ),
    )(raw_rows, length_rows, quality_rows, tables[4], tables[0], tables[1], tables[2], tables[3], tables[5])


def body(raw, lengths, quality, assignment):
    my_index = lax.axis_index("chan")
    block_rows, window_count, sample_count = raw.shape
    total_channels = assignment.shape[0]
    row_count = block_rows * window_count
    my_quality = lax.dynamic_slice_in_dim(quality, my_index * block_rows, block_rows)
    quality_rows = jnp.broadcast_to(my_quality[:, None], (block_rows, window_count))
    whitened = whitened_of(
        raw.reshape(row_count, sample_count),
        lengths.reshape(row_count, 1),
        quality_rows.reshape(row_count, 1),
    ).reshape(block_rows, window_count, 2, NB)
    panel = lax.all_to_all(whitened, "freq", split_axis=3, concat_axis=1, tiled=True)
    all_windows = panel.shape[1]
    bins_here = panel.shape[3]
    gathered = lax.all_gather(panel, "chan", axis=0, tiled=True)
    inverse = (
        jnp.zeros((total_channels,), jnp.int32)
        .at[assignment]
        .set(jnp.arange(total_channels, dtype=jnp.int32))
    )
    ordered = jnp.take(gathered, inverse, axis=0)
    mine = lax.dynamic_slice_in_dim(inverse, my_index * block_rows, block_rows)
    left = jnp.take(gathered, mine, axis=0)
    left_re = left[:, :, 0, :]
    left_im = left[:, :, 1, :]
    plain = jnp.stack([left_re, left_im], axis=1)
    turned = jnp.stack([left_im, -left_re], axis=1)
    left_rows = jnp.stack([plain, turned], axis=1)
    left_rows = left_rows.transpose(4, 0, 1, 2, 3).reshape(bins_here, block_rows * 2, 2 * all_windows)
    right = ordered.transpose(3, 2, 1, 0).reshape(bins_here, 2 * all_windows, total_channels)
    out = jnp.einsum("bik,bkj->bij", left_rows, right, preferred_element_type=jnp.float32)
    return (out / all_windows).astype(jnp.bfloat16).reshape(bins_here, block_rows, 2, total_channels)


def solution(mesh):
    return jax.shard_map(
        body,
        mesh=mesh,
        in_specs=(
            P(("groups", "chan"), "freq", None),
            P(("groups", "chan"), "freq"),
            P("groups"),
            P("groups"),
        ),
        out_specs=P("freq", ("groups", "chan"), None, None),
        check_vma=False,
    )
```

```python
import math

import numpy as np

import jax
import jax.numpy as jnp
from jax import lax
from jax.experimental import pallas as pl
from jax.experimental.pallas import tpu as pltpu
from jax.sharding import PartitionSpec as P

WIN = 12000
NB = 512
K0 = 6
SUB = 32
LANE = 128
PADDED = 12288
TILES_PER_STEP = 8


def small_table(sample_values):
    bin_index = K0 + np.arange(NB, dtype=np.int64)
    residue = sample_values[:, None] * bin_index[None, :] % WIN
    angles = residue.astype(np.float64) * (2.0 * math.pi / WIN)
    return np.cos(angles).astype(np.float32), (-np.sin(angles)).astype(np.float32)


def constant_tables():
    high_count = PADDED // LANE
    cos_high, sin_high = small_table(np.arange(high_count, dtype=np.int64) * LANE)
    cos_low, sin_low = small_table(np.arange(LANE, dtype=np.int64))
    positions = np.arange(PADDED, dtype=np.float64)
    taper = (0.5 - 0.5 * np.cos(positions * (2.0 * math.pi / WIN))).astype(np.float32)
    groups = (np.arange(NB)[:, None] // SUB == np.arange(NB // SUB)[None, :]).astype(np.float32)
    return cos_high, sin_high, cos_low, sin_low, taper.reshape(1, PADDED), groups


def dft_kernel(
    raw_ref, length_ref, quality_ref, taper_ref, cos_high_ref, sin_high_ref, cos_low_ref,
    sin_low_ref, groups_ref, out_ref, total_ref, mean_ref,
):
    phase = pl.program_id(0)
    step = pl.program_id(1)
    block = TILES_PER_STEP * LANE
    lengths = length_ref[...]

    @pl.when(jnp.logical_and(phase == 0, step == 0))
    def _():
        mean_ref[...] = jnp.zeros_like(mean_ref)
        total_ref[...] = jnp.zeros_like(total_ref)

    @pl.when(phase == 0)
    def _():
        positions = step * block + lax.broadcasted_iota(jnp.int32, raw_ref.shape, 1)
        inside = positions < lengths
        kept = jnp.where(inside, raw_ref[...].astype(jnp.float32), 0.0)
        mean_ref[...] += jnp.sum(kept, axis=1, keepdims=True)

    @pl.when(phase == 1)
    def _():
        average = mean_ref[...] / lengths.astype(jnp.float32)
        cos_low = cos_low_ref[...]
        sin_low = sin_low_ref[...]
        real_total = total_ref[:, :NB]
        imag_total = total_ref[:, NB:]
        for tile in range(TILES_PER_STEP):
            row = step * TILES_PER_STEP + tile
            cos_high = cos_high_ref[pl.ds(row, 1), :]
            sin_high = sin_high_ref[pl.ds(row, 1), :]
            cos_part = (cos_high * cos_low - sin_high * sin_low).astype(jnp.bfloat16)
            sin_part = (sin_high * cos_low + cos_high * sin_low).astype(jnp.bfloat16)
            values = raw_ref[:, tile * LANE:(tile + 1) * LANE].astype(jnp.float32)
            positions = row * LANE + lax.broadcasted_iota(jnp.int32, values.shape, 1)
            taper = taper_ref[:, pl.ds(pl.multiple_of(row * LANE, LANE), LANE)]
            samples = jnp.where(
                positions < lengths, (values - average) * taper, 0.0
            ).astype(jnp.bfloat16)
            real_total = real_total + jnp.dot(samples, cos_part, preferred_element_type=jnp.float32)
            imag_total = imag_total + jnp.dot(samples, sin_part, preferred_element_type=jnp.float32)
        total_ref[:, :NB] = real_total
        total_ref[:, NB:] = imag_total

        @pl.when(step == pl.num_programs(1) - 1)
        def _():
            groups = groups_ref[...]
            power = jnp.dot(
                real_total * real_total + imag_total * imag_total,
                groups,
                precision=lax.Precision.HIGHEST,
                preferred_element_type=jnp.float32,
            ) / SUB
            factor = lax.rsqrt(power + 1e-06)
            spread = lax.dot_general(
                factor, groups, (((1,), (1,)), ((), ())),
                precision=lax.Precision.HIGHEST,
                preferred_element_type=jnp.float32,
            )
            good = quality_ref[...] != 0
            real_out = (real_total * spread).astype(jnp.bfloat16)
            imag_out = (imag_total * spread).astype(jnp.bfloat16)
            zero = jnp.zeros_like(real_out)
            out_ref[:, :NB] = jnp.where(good, real_out, zero)
            out_ref[:, NB:] = jnp.where(good, imag_out, zero)


def whitened_of(raw_rows, length_rows, quality_rows):
    row_count = raw_rows.shape[0]
    tables = [jnp.asarray(t) for t in constant_tables()]
    block = TILES_PER_STEP * LANE
    steps = PADDED // block
    full = lambda shape: pl.BlockSpec(shape, lambda p, s: (0, 0))
    return pl.pallas_call(
        dft_kernel,
        out_shape=jax.ShapeDtypeStruct((row_count, 2 * NB), jnp.bfloat16),
        grid=(2, steps),
        in_specs=[
            pl.BlockSpec((row_count, block), lambda p, s: (0, s)),
            full((row_count, 1)),
            full((row_count, 1)),
            full((1, PADDED)),
            full(tables[1].shape),
            full(tables[1].shape),
            full(tables[2].shape),
            full(tables[2].shape),
            full(tables[5].shape),
        ],
        out_specs=full((row_count, 2 * NB)),
        scratch_shapes=[
            pltpu.VMEM((row_count, 2 * NB), jnp.float32),
            pltpu.VMEM((row_count, 1), jnp.float32),
        ],
        compiler_params=pltpu.CompilerParams(dimension_semantics=("arbitrary", "arbitrary")),
        cost_estimate=pl.CostEstimate(
            flops=2 * row_count * PADDED * 2 * NB,
            transcendentals=0,
            bytes_accessed=2 * row_count * WIN * 2 + row_count * 2 * NB * 2,
        ),
    )(raw_rows, length_rows, quality_rows, tables[4], tables[0], tables[1], tables[2], tables[3], tables[5])


def body(raw, lengths, quality, assignment):
    my_index = lax.axis_index("chan")
    block_rows, window_count, sample_count = raw.shape
    total_channels = assignment.shape[0]
    row_count = block_rows * window_count
    my_quality = lax.dynamic_slice_in_dim(quality, my_index * block_rows, block_rows)
    quality_rows = jnp.broadcast_to(my_quality[:, None], (block_rows, window_count))
    whitened = whitened_of(
        raw.reshape(row_count, sample_count),
        lengths.reshape(row_count, 1),
        quality_rows.reshape(row_count, 1),
    ).reshape(block_rows, window_count, 2, NB)
    panel = lax.all_to_all(whitened, "freq", split_axis=3, concat_axis=1, tiled=True)
    all_windows = panel.shape[1]
    bins_here = panel.shape[3]
    gathered = lax.all_gather(panel, "chan", axis=0, tiled=True)
    positions = jnp.arange(total_channels, dtype=jnp.int32)
    onehot = (assignment[:, None] == positions[None, :]).astype(jnp.bfloat16)
    right = jnp.einsum(
        "cwpb,cj->bpwj", gathered, onehot, preferred_element_type=jnp.float32
    ).astype(jnp.bfloat16).reshape(bins_here, 2 * all_windows, total_channels)
    mine = my_index * block_rows + jnp.arange(block_rows, dtype=jnp.int32)
    select = (assignment[:, None] == mine[None, :]).astype(jnp.bfloat16)
    rotation = jnp.array(
        [[[1.0, 0.0], [0.0, -1.0]], [[0.0, 1.0], [1.0, 0.0]]], dtype=jnp.bfloat16
    )
    spread = select[:, None, :, None, None] * rotation[None, :, None, :, :]
    left_rows = jnp.einsum(
        "cwpb,cpiqr->biqrw", gathered, spread, preferred_element_type=jnp.float32
    ).astype(jnp.bfloat16).reshape(bins_here, block_rows * 2, 2 * all_windows)
    out = jnp.einsum("bik,bkj->bij", left_rows, right, preferred_element_type=jnp.float32)
    return (out / all_windows).astype(jnp.bfloat16).reshape(bins_here, block_rows, 2, total_channels)


def solution(mesh):
    return jax.shard_map(
        body,
        mesh=mesh,
        in_specs=(
            P(("groups", "chan"), "freq", None),
            P(("groups", "chan"), "freq"),
            P("groups"),
            P("groups"),
        ),
        out_specs=P("freq", ("groups", "chan"), None, None),
        check_vma=False,
    )
```

```python
import functools
import math

import numpy as np

import jax
import jax.numpy as jnp
from jax import lax
from jax.experimental import pallas as pl
from jax.experimental.pallas import tpu as pltpu
from jax.sharding import PartitionSpec as P

WIN = 12000
NB = 512
K0 = 6
SUB = 32
LANE = 128
PADDED = 12288
TILES_PER_STEP = 8


def small_table(sample_values):
    bin_index = K0 + np.arange(NB, dtype=np.int64)
    residue = sample_values[:, None] * bin_index[None, :] % WIN
    angles = residue.astype(np.float64) * (2.0 * math.pi / WIN)
    return np.cos(angles).astype(np.float32), (-np.sin(angles)).astype(np.float32)


def constant_tables():
    high_count = PADDED // LANE
    cos_high, sin_high = small_table(np.arange(high_count, dtype=np.int64) * LANE)
    cos_low, sin_low = small_table(np.arange(LANE, dtype=np.int64))
    positions = np.arange(PADDED, dtype=np.float64)
    taper = (0.5 - 0.5 * np.cos(positions * (2.0 * math.pi / WIN))).astype(np.float32)
    groups = (np.arange(NB)[:, None] // SUB == np.arange(NB // SUB)[None, :]).astype(np.float32)
    return cos_high, sin_high, cos_low, sin_low, taper.reshape(1, PADDED), groups


def dft_kernel(
    raw_ref, length_ref, quality_ref, taper_ref, cos_high_ref, sin_high_ref, cos_low_ref,
    sin_low_ref, groups_ref, out_ref, total_ref, mean_ref,
):
    phase = pl.program_id(0)
    step = pl.program_id(1)
    block = TILES_PER_STEP * LANE
    lengths = length_ref[...]

    @pl.when(jnp.logical_and(phase == 0, step == 0))
    def _():
        mean_ref[...] = jnp.zeros_like(mean_ref)
        total_ref[...] = jnp.zeros_like(total_ref)

    @pl.when(phase == 0)
    def _():
        positions = step * block + lax.broadcasted_iota(jnp.int32, raw_ref.shape, 1)
        inside = positions < lengths
        kept = jnp.where(inside, raw_ref[...].astype(jnp.float32), 0.0)
        mean_ref[...] += jnp.sum(kept, axis=1, keepdims=True)

    @pl.when(phase == 1)
    def _():
        average = mean_ref[...] / lengths.astype(jnp.float32)
        cos_low = cos_low_ref[...]
        sin_low = sin_low_ref[...]
        real_total = total_ref[:, :NB]
        imag_total = total_ref[:, NB:]
        for tile in range(TILES_PER_STEP):
            row = step * TILES_PER_STEP + tile
            cos_high = cos_high_ref[pl.ds(row, 1), :]
            sin_high = sin_high_ref[pl.ds(row, 1), :]
            cos_part = (cos_high * cos_low - sin_high * sin_low).astype(jnp.bfloat16)
            sin_part = (sin_high * cos_low + cos_high * sin_low).astype(jnp.bfloat16)
            values = raw_ref[:, tile * LANE:(tile + 1) * LANE].astype(jnp.float32)
            positions = row * LANE + lax.broadcasted_iota(jnp.int32, values.shape, 1)
            taper = taper_ref[:, pl.ds(pl.multiple_of(row * LANE, LANE), LANE)]
            samples = jnp.where(
                positions < lengths, (values - average) * taper, 0.0
            ).astype(jnp.bfloat16)
            real_total = real_total + jnp.dot(samples, cos_part, preferred_element_type=jnp.float32)
            imag_total = imag_total + jnp.dot(samples, sin_part, preferred_element_type=jnp.float32)
        total_ref[:, :NB] = real_total
        total_ref[:, NB:] = imag_total

        @pl.when(step == pl.num_programs(1) - 1)
        def _():
            groups = groups_ref[...]
            power = jnp.dot(
                real_total * real_total + imag_total * imag_total,
                groups,
                precision=lax.Precision.HIGHEST,
                preferred_element_type=jnp.float32,
            ) / SUB
            factor = lax.rsqrt(power + 1e-06)
            spread = lax.dot_general(
                factor, groups, (((1,), (1,)), ((), ())),
                precision=lax.Precision.HIGHEST,
                preferred_element_type=jnp.float32,
            )
            good = quality_ref[...] != 0
            real_out = (real_total * spread).astype(jnp.bfloat16)
            imag_out = (imag_total * spread).astype(jnp.bfloat16)
            zero = jnp.zeros_like(real_out)
            out_ref[:, :NB] = jnp.where(good, real_out, zero)
            out_ref[:, NB:] = jnp.where(good, imag_out, zero)


def whitened_of(raw_rows, length_rows, quality_rows):
    row_count = raw_rows.shape[0]
    tables = [jnp.asarray(t) for t in constant_tables()]
    block = TILES_PER_STEP * LANE
    steps = PADDED // block
    full = lambda shape: pl.BlockSpec(shape, lambda p, s: (0, 0))
    return pl.pallas_call(
        dft_kernel,
        out_shape=jax.ShapeDtypeStruct((row_count, 2 * NB), jnp.bfloat16),
        grid=(2, steps),
        in_specs=[
            pl.BlockSpec((row_count, block), lambda p, s: (0, s)),
            full((row_count, 1)),
            full((row_count, 1)),
            full((1, PADDED)),
            full(tables[1].shape),
            full(tables[1].shape),
            full(tables[2].shape),
            full(tables[2].shape),
            full(tables[5].shape),
        ],
        out_specs=full((row_count, 2 * NB)),
        scratch_shapes=[
            pltpu.VMEM((row_count, 2 * NB), jnp.float32),
            pltpu.VMEM((row_count, 1), jnp.float32),
        ],
        compiler_params=pltpu.CompilerParams(dimension_semantics=("arbitrary", "arbitrary")),
        cost_estimate=pl.CostEstimate(
            flops=2 * row_count * PADDED * 2 * NB,
            transcendentals=0,
            bytes_accessed=2 * row_count * WIN * 2 + row_count * 2 * NB * 2,
        ),
    )(raw_rows, length_rows, quality_rows, tables[4], tables[0], tables[1], tables[2], tables[3], tables[5])


def device_index(z, y, core):
    return z * 4 + y * 2 + core


def across(valid):
    return [
        (device_index(z, y, core), device_index(z, 1 - y, core))
        for z in range(4) if valid(z) for y in range(2) for core in range(2)
    ]


def compact(own, ups, downs, z):
    line = jnp.zeros((4,) + own.shape, own.dtype)
    for hop in (3, 2, 1):
        line = lax.dynamic_update_index_in_dim(line, ups[hop - 1], jnp.maximum(z - hop, 0), 0)
    for hop in (3, 2, 1):
        line = lax.dynamic_update_index_in_dim(line, downs[hop - 1], jnp.minimum(z + hop, 3), 0)
    return lax.dynamic_update_index_in_dim(line, own, z, 0)


def line_gather(block):
    me = lax.axis_index("chan")
    z = me // 4
    y = (me // 2) % 2
    core = me % 2
    up = [(device_index(a, b, c), device_index(a + 1, b, c)) for a in range(3) for b in range(2) for c in range(2)]
    down = [(device_index(a, b, c), device_index(a - 1, b, c)) for a in range(1, 4) for b in range(2) for c in range(2)]
    other_own = lax.ppermute(block, "chan", across(lambda a: True))
    ups, downs, other_ups, other_downs = [], [], [], []
    going_up = going_down = block
    for hop in range(1, 4):
        going_up = lax.ppermute(going_up, "chan", up)
        going_down = lax.ppermute(going_down, "chan", down)
        ups.append(going_up)
        downs.append(going_down)
        other_ups.append(lax.ppermute(going_up, "chan", across(lambda a, h=hop: a >= h)))
        other_downs.append(lax.ppermute(going_down, "chan", across(lambda a, h=hop: a + h <= 3)))
    both = jnp.concatenate(
        [compact(block, ups, downs, z), compact(other_own, other_ups, other_downs, z)], 0
    )
    sibling = lax.ppermute(both, "chan", [(i, i ^ 1) for i in range(16)])
    gathered = jnp.concatenate([both, sibling], 0)
    slots = jnp.arange(16, dtype=jnp.int32)
    part = slots // 4
    slot_y = jnp.where(part % 2 == 0, y, 1 - y)
    slot_core = jnp.where(part < 2, core, 1 - core)
    owner = device_index(slots % 4, slot_y, slot_core)
    return gathered.reshape((16 * block.shape[0],) + block.shape[1:]), owner


def body(use_lines, raw, lengths, quality, assignment):
    my_index = lax.axis_index("chan")
    block_rows, window_count, sample_count = raw.shape
    total_channels = assignment.shape[0]
    row_count = block_rows * window_count
    my_quality = lax.dynamic_slice_in_dim(quality, my_index * block_rows, block_rows)
    quality_rows = jnp.broadcast_to(my_quality[:, None], (block_rows, window_count))
    whitened = whitened_of(
        raw.reshape(row_count, sample_count),
        lengths.reshape(row_count, 1),
        quality_rows.reshape(row_count, 1),
    ).reshape(block_rows, window_count, 2, NB)
    panel = lax.all_to_all(whitened, "freq", split_axis=3, concat_axis=1, tiled=True)
    all_windows = panel.shape[1]
    bins_here = panel.shape[3]
    if use_lines:
        gathered, owner = line_gather(panel)
        rows = jnp.arange(block_rows, dtype=jnp.int32)
        slot_channel = (owner[:, None] * block_rows + rows[None, :]).reshape(total_channels)
        slot_assignment = jnp.take(assignment, slot_channel)
    else:
        gathered = lax.all_gather(panel, "chan", axis=0, tiled=True)
        slot_assignment = assignment
    positions = jnp.arange(total_channels, dtype=jnp.int32)
    onehot = (slot_assignment[:, None] == positions[None, :]).astype(jnp.bfloat16)
    right = jnp.einsum(
        "cwpb,cj->bpwj", gathered, onehot, preferred_element_type=jnp.float32
    ).astype(jnp.bfloat16).reshape(bins_here, 2 * all_windows, total_channels)
    mine = my_index * block_rows + jnp.arange(block_rows, dtype=jnp.int32)
    select = (slot_assignment[:, None] == mine[None, :]).astype(jnp.bfloat16)
    rotation = jnp.array(
        [[[1.0, 0.0], [0.0, -1.0]], [[0.0, 1.0], [1.0, 0.0]]], dtype=jnp.bfloat16
    )
    spread = select[:, None, :, None, None] * rotation[None, :, None, :, :]
    left_rows = jnp.einsum(
        "cwpb,cpiqr->biqrw", gathered, spread, preferred_element_type=jnp.float32
    ).astype(jnp.bfloat16).reshape(bins_here, block_rows * 2, 2 * all_windows)
    out = jnp.einsum("bik,bkj->bij", left_rows, right, preferred_element_type=jnp.float32)
    return (out / all_windows).astype(jnp.bfloat16).reshape(bins_here, block_rows, 2, total_channels)


def lines_fit(mesh):
    if dict(mesh.shape) != {"groups": mesh.shape["groups"], "chan": 16, "freq": 1}:
        return False
    devices = mesh.devices.reshape(mesh.shape["groups"], 16)
    for group in devices:
        first = getattr(group[0], "coords", None)
        if first is None:
            return False
        for position, device in enumerate(group):
            z, y, core = position // 4, (position // 2) % 2, position % 2
            where = tuple(device.coords)
            if getattr(device, "core_on_chip", None) != core:
                return False
            if where != (first[0], first[1] + y, first[2] + z):
                return False
    return True


def solution(mesh):
    return jax.shard_map(
        functools.partial(body, lines_fit(mesh)),
        mesh=mesh,
        in_specs=(
            P(("groups", "chan"), "freq", None),
            P(("groups", "chan"), "freq"),
            P("groups"),
            P("groups"),
        ),
        out_specs=P("freq", ("groups", "chan"), None, None),
        check_vma=False,
    )
```

```python
import functools
import math

import numpy as np

import jax
import jax.numpy as jnp
from jax import lax
from jax.experimental import pallas as pl
from jax.experimental.pallas import tpu as pltpu
from jax.sharding import PartitionSpec as P

WIN = 12000
NB = 512
K0 = 6
SUB = 32
LANE = 128
PADDED = 12288
TILES_PER_STEP = 16


def small_table(sample_values):
    bin_index = K0 + np.arange(NB, dtype=np.int64)
    residue = sample_values[:, None] * bin_index[None, :] % WIN
    angles = residue.astype(np.float64) * (2.0 * math.pi / WIN)
    return np.cos(angles).astype(np.float32), (-np.sin(angles)).astype(np.float32)


def constant_tables():
    high_count = PADDED // LANE
    cos_high, sin_high = small_table(np.arange(high_count, dtype=np.int64) * LANE)
    cos_low, sin_low = small_table(np.arange(LANE, dtype=np.int64))
    positions = np.arange(PADDED, dtype=np.float64)
    taper = (0.5 - 0.5 * np.cos(positions * (2.0 * math.pi / WIN))).astype(np.float32)
    groups = (np.arange(NB)[:, None] // SUB == np.arange(NB // SUB)[None, :]).astype(np.float32)
    return cos_high, sin_high, cos_low, sin_low, taper.reshape(1, PADDED), groups


def dft_kernel(
    raw_ref, length_ref, quality_ref, taper_ref, cos_high_ref, sin_high_ref, cos_low_ref,
    sin_low_ref, groups_ref, out_ref, total_ref, mean_ref,
):
    phase = pl.program_id(0)
    step = pl.program_id(1)
    block = TILES_PER_STEP * LANE
    lengths = length_ref[...]

    @pl.when(jnp.logical_and(phase == 0, step == 0))
    def _():
        mean_ref[...] = jnp.zeros_like(mean_ref)
        total_ref[...] = jnp.zeros_like(total_ref)

    @pl.when(phase == 0)
    def _():
        positions = step * block + lax.broadcasted_iota(jnp.int32, raw_ref.shape, 1)
        inside = positions < lengths
        kept = jnp.where(inside, raw_ref[...].astype(jnp.float32), 0.0)
        mean_ref[...] += jnp.sum(kept, axis=1, keepdims=True)

    @pl.when(phase == 1)
    def _():
        average = mean_ref[...] / lengths.astype(jnp.float32)
        cos_low = cos_low_ref[...]
        sin_low = sin_low_ref[...]
        real_total = total_ref[:, :NB]
        imag_total = total_ref[:, NB:]
        for tile in range(TILES_PER_STEP):
            row = step * TILES_PER_STEP + tile
            cos_high = cos_high_ref[pl.ds(row, 1), :]
            sin_high = sin_high_ref[pl.ds(row, 1), :]
            cos_part = (cos_high * cos_low - sin_high * sin_low).astype(jnp.bfloat16)
            sin_part = (sin_high * cos_low + cos_high * sin_low).astype(jnp.bfloat16)
            values = raw_ref[:, tile * LANE:(tile + 1) * LANE].astype(jnp.float32)
            positions = row * LANE + lax.broadcasted_iota(jnp.int32, values.shape, 1)
            taper = taper_ref[:, pl.ds(pl.multiple_of(row * LANE, LANE), LANE)]
            samples = jnp.where(
                positions < lengths, (values - average) * taper, 0.0
            ).astype(jnp.bfloat16)
            real_total = real_total + jnp.dot(samples, cos_part, preferred_element_type=jnp.float32)
            imag_total = imag_total + jnp.dot(samples, sin_part, preferred_element_type=jnp.float32)
        total_ref[:, :NB] = real_total
        total_ref[:, NB:] = imag_total

        @pl.when(step == pl.num_programs(1) - 1)
        def _():
            groups = groups_ref[...]
            power = jnp.dot(
                real_total * real_total + imag_total * imag_total,
                groups,
                precision=lax.Precision.HIGHEST,
                preferred_element_type=jnp.float32,
            ) / SUB
            factor = lax.rsqrt(power + 1e-06)
            spread = lax.dot_general(
                factor, groups, (((1,), (1,)), ((), ())),
                precision=lax.Precision.HIGHEST,
                preferred_element_type=jnp.float32,
            )
            good = quality_ref[...] != 0
            real_out = (real_total * spread).astype(jnp.bfloat16)
            imag_out = (imag_total * spread).astype(jnp.bfloat16)
            zero = jnp.zeros_like(real_out)
            out_ref[:, :NB] = jnp.where(good, real_out, zero)
            out_ref[:, NB:] = jnp.where(good, imag_out, zero)


def whitened_of(raw_rows, length_rows, quality_rows):
    row_count = raw_rows.shape[0]
    tables = [jnp.asarray(t) for t in constant_tables()]
    block = TILES_PER_STEP * LANE
    steps = PADDED // block
    full = lambda shape: pl.BlockSpec(shape, lambda p, s: (0, 0))
    return pl.pallas_call(
        dft_kernel,
        out_shape=jax.ShapeDtypeStruct((row_count, 2 * NB), jnp.bfloat16),
        grid=(2, steps),
        in_specs=[
            pl.BlockSpec((row_count, block), lambda p, s: (0, s)),
            full((row_count, 1)),
            full((row_count, 1)),
            full((1, PADDED)),
            full(tables[1].shape),
            full(tables[1].shape),
            full(tables[2].shape),
            full(tables[2].shape),
            full(tables[5].shape),
        ],
        out_specs=full((row_count, 2 * NB)),
        scratch_shapes=[
            pltpu.VMEM((row_count, 2 * NB), jnp.float32),
            pltpu.VMEM((row_count, 1), jnp.float32),
        ],
        compiler_params=pltpu.CompilerParams(dimension_semantics=("arbitrary", "arbitrary")),
        cost_estimate=pl.CostEstimate(
            flops=2 * row_count * PADDED * 2 * NB,
            transcendentals=0,
            bytes_accessed=2 * row_count * WIN * 2 + row_count * 2 * NB * 2,
        ),
    )(raw_rows, length_rows, quality_rows, tables[4], tables[0], tables[1], tables[2], tables[3], tables[5])


def device_index(z, y, core):
    return z * 4 + y * 2 + core


def across(valid):
    return [
        (device_index(z, y, core), device_index(z, 1 - y, core))
        for z in range(4) if valid(z) for y in range(2) for core in range(2)
    ]


def compact(own, ups, downs, z):
    line = jnp.zeros((4,) + own.shape, own.dtype)
    for hop in (3, 2, 1):
        line = lax.dynamic_update_index_in_dim(line, ups[hop - 1], jnp.maximum(z - hop, 0), 0)
    for hop in (3, 2, 1):
        line = lax.dynamic_update_index_in_dim(line, downs[hop - 1], jnp.minimum(z + hop, 3), 0)
    return lax.dynamic_update_index_in_dim(line, own, z, 0)


def line_gather(block):
    me = lax.axis_index("chan")
    z = me // 4
    y = (me // 2) % 2
    core = me % 2
    up = [(device_index(a, b, c), device_index(a + 1, b, c)) for a in range(3) for b in range(2) for c in range(2)]
    down = [(device_index(a, b, c), device_index(a - 1, b, c)) for a in range(1, 4) for b in range(2) for c in range(2)]
    other_own = lax.ppermute(block, "chan", across(lambda a: True))
    ups, downs, other_ups, other_downs = [], [], [], []
    going_up = going_down = block
    for hop in range(1, 4):
        going_up = lax.ppermute(going_up, "chan", up)
        going_down = lax.ppermute(going_down, "chan", down)
        ups.append(going_up)
        downs.append(going_down)
        other_ups.append(lax.ppermute(going_up, "chan", across(lambda a, h=hop: a >= h)))
        other_downs.append(lax.ppermute(going_down, "chan", across(lambda a, h=hop: a + h <= 3)))
    both = jnp.concatenate(
        [compact(block, ups, downs, z), compact(other_own, other_ups, other_downs, z)], 0
    )
    sibling = lax.ppermute(both, "chan", [(i, i ^ 1) for i in range(16)])
    gathered = jnp.concatenate([both, sibling], 0)
    slots = jnp.arange(16, dtype=jnp.int32)
    part = slots // 4
    slot_y = jnp.where(part % 2 == 0, y, 1 - y)
    slot_core = jnp.where(part < 2, core, 1 - core)
    owner = device_index(slots % 4, slot_y, slot_core)
    return gathered.reshape((16 * block.shape[0],) + block.shape[1:]), owner


def body(use_lines, raw, lengths, quality, assignment):
    my_index = lax.axis_index("chan")
    block_rows, window_count, sample_count = raw.shape
    total_channels = assignment.shape[0]
    row_count = block_rows * window_count
    my_quality = lax.dynamic_slice_in_dim(quality, my_index * block_rows, block_rows)
    quality_rows = jnp.broadcast_to(my_quality[:, None], (block_rows, window_count))
    whitened = whitened_of(
        raw.reshape(row_count, sample_count),
        lengths.reshape(row_count, 1),
        quality_rows.reshape(row_count, 1),
    ).reshape(block_rows, window_count, 2, NB)
    panel = lax.all_to_all(whitened, "freq", split_axis=3, concat_axis=1, tiled=True)
    all_windows = panel.shape[1]
    bins_here = panel.shape[3]
    if use_lines:
        gathered, owner = line_gather(panel)
        rows = jnp.arange(block_rows, dtype=jnp.int32)
        slot_channel = (owner[:, None] * block_rows + rows[None, :]).reshape(total_channels)
        slot_assignment = jnp.take(assignment, slot_channel)
    else:
        gathered = lax.all_gather(panel, "chan", axis=0, tiled=True)
        slot_assignment = assignment
    positions = jnp.arange(total_channels, dtype=jnp.int32)
    onehot = (slot_assignment[:, None] == positions[None, :]).astype(jnp.bfloat16)
    right = jnp.einsum(
        "cwpb,cj->bpwj", gathered, onehot, preferred_element_type=jnp.float32
    ).astype(jnp.bfloat16).reshape(bins_here, 2 * all_windows, total_channels)
    mine = my_index * block_rows + jnp.arange(block_rows, dtype=jnp.int32)
    select = (slot_assignment[:, None] == mine[None, :]).astype(jnp.bfloat16)
    rotation = jnp.array(
        [[[1.0, 0.0], [0.0, -1.0]], [[0.0, 1.0], [1.0, 0.0]]], dtype=jnp.bfloat16
    )
    spread = select[:, None, :, None, None] * rotation[None, :, None, :, :]
    left_rows = jnp.einsum(
        "cwpb,cpiqr->biqrw", gathered, spread, preferred_element_type=jnp.float32
    ).astype(jnp.bfloat16).reshape(bins_here, block_rows * 2, 2 * all_windows)
    out = jnp.einsum("bik,bkj->bij", left_rows, right, preferred_element_type=jnp.float32)
    return (out / all_windows).astype(jnp.bfloat16).reshape(bins_here, block_rows, 2, total_channels)


def lines_fit(mesh):
    if dict(mesh.shape) != {"groups": mesh.shape["groups"], "chan": 16, "freq": 1}:
        return False
    devices = mesh.devices.reshape(mesh.shape["groups"], 16)
    for group in devices:
        first = getattr(group[0], "coords", None)
        if first is None:
            return False
        for position, device in enumerate(group):
            z, y, core = position // 4, (position // 2) % 2, position % 2
            where = tuple(device.coords)
            if getattr(device, "core_on_chip", None) != core:
                return False
            if where != (first[0], first[1] + y, first[2] + z):
                return False
    return True


def solution(mesh):
    return jax.shard_map(
        functools.partial(body, lines_fit(mesh)),
        mesh=mesh,
        in_specs=(
            P(("groups", "chan"), "freq", None),
            P(("groups", "chan"), "freq"),
            P("groups"),
            P("groups"),
        ),
        out_specs=P("freq", ("groups", "chan"), None, None),
        check_vma=False,
    )
```

```python
import functools
import math

import numpy as np

import jax
import jax.numpy as jnp
from jax import lax
from jax.experimental import pallas as pl
from jax.experimental.pallas import tpu as pltpu
from jax.sharding import PartitionSpec as P

WIN = 12000
NB = 512
K0 = 6
SUB = 32
LANE = 128
PADDED = 12288
TILES_PER_STEP = 24


def small_table(sample_values):
    bin_index = K0 + np.arange(NB, dtype=np.int64)
    residue = sample_values[:, None] * bin_index[None, :] % WIN
    angles = residue.astype(np.float64) * (2.0 * math.pi / WIN)
    return np.cos(angles).astype(np.float32), (-np.sin(angles)).astype(np.float32)


def constant_tables():
    high_count = PADDED // LANE
    cos_high, sin_high = small_table(np.arange(high_count, dtype=np.int64) * LANE)
    cos_low, sin_low = small_table(np.arange(LANE, dtype=np.int64))
    positions = np.arange(PADDED, dtype=np.float64)
    taper = (0.5 - 0.5 * np.cos(positions * (2.0 * math.pi / WIN))).astype(np.float32)
    groups = (np.arange(NB)[:, None] // SUB == np.arange(NB // SUB)[None, :]).astype(np.float32)
    return cos_high, sin_high, cos_low, sin_low, taper.reshape(1, PADDED), groups


def dft_kernel(
    raw_ref, code_ref, taper_ref, cos_high_ref, sin_high_ref, cos_low_ref,
    sin_low_ref, groups_ref, out_ref, total_ref, mean_ref,
):
    phase = pl.program_id(0)
    step = pl.program_id(1)
    block = TILES_PER_STEP * LANE
    codes = code_ref[...]
    lengths = codes // 2

    @pl.when(jnp.logical_and(phase == 0, step == 0))
    def _():
        mean_ref[...] = jnp.zeros_like(mean_ref)
        total_ref[...] = jnp.zeros_like(total_ref)

    @pl.when(phase == 0)
    def _():
        positions = step * block + lax.broadcasted_iota(jnp.int32, raw_ref.shape, 1)
        inside = positions < lengths
        kept = jnp.where(inside, raw_ref[...].astype(jnp.float32), 0.0)
        mean_ref[...] += jnp.sum(kept, axis=1, keepdims=True)

    @pl.when(phase == 1)
    def _():
        average = mean_ref[...] / lengths.astype(jnp.float32)
        cos_low = cos_low_ref[...]
        sin_low = sin_low_ref[...]
        real_total = total_ref[:, :NB]
        imag_total = total_ref[:, NB:]
        for tile in range(TILES_PER_STEP):
            row = step * TILES_PER_STEP + tile
            cos_high = cos_high_ref[pl.ds(row, 1), :]
            sin_high = sin_high_ref[pl.ds(row, 1), :]
            cos_part = (cos_high * cos_low - sin_high * sin_low).astype(jnp.bfloat16)
            sin_part = (sin_high * cos_low + cos_high * sin_low).astype(jnp.bfloat16)
            values = raw_ref[:, tile * LANE:(tile + 1) * LANE].astype(jnp.float32)
            positions = row * LANE + lax.broadcasted_iota(jnp.int32, values.shape, 1)
            taper = taper_ref[:, pl.ds(pl.multiple_of(row * LANE, LANE), LANE)]
            samples = jnp.where(
                positions < lengths, (values - average) * taper, 0.0
            ).astype(jnp.bfloat16)
            real_total = real_total + jnp.dot(samples, cos_part, preferred_element_type=jnp.float32)
            imag_total = imag_total + jnp.dot(samples, sin_part, preferred_element_type=jnp.float32)
        total_ref[:, :NB] = real_total
        total_ref[:, NB:] = imag_total

        @pl.when(step == pl.num_programs(1) - 1)
        def _():
            groups = groups_ref[...]
            power = jnp.dot(
                real_total * real_total + imag_total * imag_total,
                groups,
                precision=lax.Precision.HIGHEST,
                preferred_element_type=jnp.float32,
            ) / SUB
            factor = lax.rsqrt(power + 1e-06)
            spread = lax.dot_general(
                factor, groups, (((1,), (1,)), ((), ())),
                precision=lax.Precision.HIGHEST,
                preferred_element_type=jnp.float32,
            )
            good = codes % 2 != 0
            real_out = (real_total * spread).astype(jnp.bfloat16)
            imag_out = (imag_total * spread).astype(jnp.bfloat16)
            zero = jnp.zeros_like(real_out)
            out_ref[:, :NB] = jnp.where(good, real_out, zero)
            out_ref[:, NB:] = jnp.where(good, imag_out, zero)


def whitened_of(raw_rows, code_rows):
    row_count = raw_rows.shape[0]
    tables = [jnp.asarray(t) for t in constant_tables()]
    block = TILES_PER_STEP * LANE
    steps = PADDED // block
    full = lambda shape: pl.BlockSpec(shape, lambda p, s: (0, 0))
    return pl.pallas_call(
        dft_kernel,
        out_shape=jax.ShapeDtypeStruct((row_count, 2 * NB), jnp.bfloat16),
        grid=(2, steps),
        in_specs=[
            pl.BlockSpec((row_count, block), lambda p, s: (0, s)),
            full((row_count, 1)),
            full((1, PADDED)),
            full(tables[1].shape),
            full(tables[1].shape),
            full(tables[2].shape),
            full(tables[2].shape),
            full(tables[5].shape),
        ],
        out_specs=full((row_count, 2 * NB)),
        scratch_shapes=[
            pltpu.VMEM((row_count, 2 * NB), jnp.float32),
            pltpu.VMEM((row_count, 1), jnp.float32),
        ],
        compiler_params=pltpu.CompilerParams(dimension_semantics=("arbitrary", "arbitrary")),
        cost_estimate=pl.CostEstimate(
            flops=2 * row_count * PADDED * 2 * NB,
            transcendentals=0,
            bytes_accessed=2 * row_count * WIN * 2 + row_count * 2 * NB * 2,
        ),
    )(raw_rows, code_rows, tables[4], tables[0], tables[1], tables[2], tables[3], tables[5])


def device_index(z, y, core):
    return z * 4 + y * 2 + core


def across(valid):
    return [
        (device_index(z, y, core), device_index(z, 1 - y, core))
        for z in range(4) if valid(z) for y in range(2) for core in range(2)
    ]


def compact(own, ups, downs, z):
    line = jnp.zeros((4,) + own.shape, own.dtype)
    for hop in (3, 2, 1):
        line = lax.dynamic_update_index_in_dim(line, ups[hop - 1], jnp.maximum(z - hop, 0), 0)
    for hop in (3, 2, 1):
        line = lax.dynamic_update_index_in_dim(line, downs[hop - 1], jnp.minimum(z + hop, 3), 0)
    return lax.dynamic_update_index_in_dim(line, own, z, 0)


def line_gather(block):
    me = lax.axis_index("chan")
    z = me // 4
    y = (me // 2) % 2
    core = me % 2
    up = [(device_index(a, b, c), device_index(a + 1, b, c)) for a in range(3) for b in range(2) for c in range(2)]
    down = [(device_index(a, b, c), device_index(a - 1, b, c)) for a in range(1, 4) for b in range(2) for c in range(2)]
    other_own = lax.ppermute(block, "chan", across(lambda a: True))
    ups, downs, other_ups, other_downs = [], [], [], []
    going_up = going_down = block
    for hop in range(1, 4):
        going_up = lax.ppermute(going_up, "chan", up)
        going_down = lax.ppermute(going_down, "chan", down)
        ups.append(going_up)
        downs.append(going_down)
        other_ups.append(lax.ppermute(going_up, "chan", across(lambda a, h=hop: a >= h)))
        other_downs.append(lax.ppermute(going_down, "chan", across(lambda a, h=hop: a + h <= 3)))
    both = jnp.concatenate(
        [compact(block, ups, downs, z), compact(other_own, other_ups, other_downs, z)], 0
    )
    sibling = lax.ppermute(both, "chan", [(i, i ^ 1) for i in range(16)])
    gathered = jnp.concatenate([both, sibling], 0)
    slots = jnp.arange(16, dtype=jnp.int32)
    part = slots // 4
    slot_y = jnp.where(part % 2 == 0, y, 1 - y)
    slot_core = jnp.where(part < 2, core, 1 - core)
    owner = device_index(slots % 4, slot_y, slot_core)
    return gathered.reshape((16 * block.shape[0],) + block.shape[1:]), owner


def body(use_lines, raw, lengths, quality, assignment):
    my_index = lax.axis_index("chan")
    block_rows, window_count, sample_count = raw.shape
    total_channels = assignment.shape[0]
    row_count = block_rows * window_count
    my_quality = lax.dynamic_slice_in_dim(quality, my_index * block_rows, block_rows)
    codes = lengths * 2 + (my_quality[:, None] != 0).astype(jnp.int32)
    whitened = whitened_of(
        raw.reshape(row_count, sample_count), codes.reshape(row_count, 1)
    ).reshape(block_rows, window_count, 2, NB)
    panel = lax.all_to_all(whitened, "freq", split_axis=3, concat_axis=1, tiled=True)
    all_windows = panel.shape[1]
    bins_here = panel.shape[3]
    if use_lines:
        gathered, owner = line_gather(panel)
        rows = jnp.arange(block_rows, dtype=jnp.int32)
        slot_channel = (owner[:, None] * block_rows + rows[None, :]).reshape(total_channels)
        slot_assignment = jnp.take(assignment, slot_channel)
    else:
        gathered = lax.all_gather(panel, "chan", axis=0, tiled=True)
        slot_assignment = assignment
    positions = jnp.arange(total_channels, dtype=jnp.int32)
    onehot = (slot_assignment[:, None] == positions[None, :]).astype(jnp.bfloat16)
    right = jnp.einsum(
        "cwpb,cj->bpwj", gathered, onehot, preferred_element_type=jnp.float32
    ).astype(jnp.bfloat16).reshape(bins_here, 2 * all_windows, total_channels)
    mine = my_index * block_rows + jnp.arange(block_rows, dtype=jnp.int32)
    select = (slot_assignment[:, None] == mine[None, :]).astype(jnp.bfloat16)
    rotation = jnp.array(
        [[[1.0, 0.0], [0.0, -1.0]], [[0.0, 1.0], [1.0, 0.0]]], dtype=jnp.bfloat16
    )
    spread = select[:, None, :, None, None] * rotation[None, :, None, :, :]
    left_rows = jnp.einsum(
        "cwpb,cpiqr->biqrw", gathered, spread, preferred_element_type=jnp.float32
    ).astype(jnp.bfloat16).reshape(bins_here, block_rows * 2, 2 * all_windows)
    out = jnp.einsum("bik,bkj->bij", left_rows, right, preferred_element_type=jnp.float32)
    return (out / all_windows).astype(jnp.bfloat16).reshape(bins_here, block_rows, 2, total_channels)


def lines_fit(mesh):
    if dict(mesh.shape) != {"groups": mesh.shape["groups"], "chan": 16, "freq": 1}:
        return False
    devices = mesh.devices.reshape(mesh.shape["groups"], 16)
    for group in devices:
        first = getattr(group[0], "coords", None)
        if first is None:
            return False
        for position, device in enumerate(group):
            z, y, core = position // 4, (position // 2) % 2, position % 2
            where = tuple(device.coords)
            if getattr(device, "core_on_chip", None) != core:
                return False
            if where != (first[0], first[1] + y, first[2] + z):
                return False
    return True


def solution(mesh):
    return jax.shard_map(
        functools.partial(body, lines_fit(mesh)),
        mesh=mesh,
        in_specs=(
            P(("groups", "chan"), "freq", None),
            P(("groups", "chan"), "freq"),
            P("groups"),
            P("groups"),
        ),
        out_specs=P("freq", ("groups", "chan"), None, None),
        check_vma=False,
    )
```

```python
import functools
import math

import numpy as np

import jax
import jax.numpy as jnp
from jax import lax
from jax.experimental import pallas as pl
from jax.experimental.pallas import tpu as pltpu
from jax.sharding import PartitionSpec as P

WIN = 12000
NB = 512
K0 = 6
SUB = 32
LANE = 128
PADDED = 12288
TILES_PER_STEP = 24


def small_table(sample_values):
    bin_index = K0 + np.arange(NB, dtype=np.int64)
    residue = sample_values[:, None] * bin_index[None, :] % WIN
    angles = residue.astype(np.float64) * (2.0 * math.pi / WIN)
    return np.cos(angles).astype(np.float32), (-np.sin(angles)).astype(np.float32)


def constant_tables():
    high_count = PADDED // LANE
    cos_high, sin_high = small_table(np.arange(high_count, dtype=np.int64) * LANE)
    cos_low, sin_low = small_table(np.arange(LANE, dtype=np.int64))
    positions = np.arange(PADDED, dtype=np.float64)
    taper = (0.5 - 0.5 * np.cos(positions * (2.0 * math.pi / WIN))).astype(np.float32)
    groups = (np.arange(NB)[:, None] // SUB == np.arange(NB // SUB)[None, :]).astype(np.float32)
    return cos_high, sin_high, cos_low, sin_low, taper.reshape(1, PADDED), groups


def dft_kernel(
    raw_ref, code_ref, taper_ref, cos_high_ref, sin_high_ref, cos_low_ref,
    sin_low_ref, groups_ref, out_ref, total_ref, mean_ref,
):
    phase = pl.program_id(0)
    step = pl.program_id(1)
    block = TILES_PER_STEP * LANE
    codes = code_ref[...]
    lengths = codes // 2

    @pl.when(jnp.logical_and(phase == 0, step == 0))
    def _():
        mean_ref[...] = jnp.zeros_like(mean_ref)
        total_ref[...] = jnp.zeros_like(total_ref)

    @pl.when(phase == 0)
    def _():
        positions = step * block + lax.broadcasted_iota(jnp.int32, raw_ref.shape, 1)
        inside = positions < lengths
        kept = jnp.where(inside, raw_ref[...].astype(jnp.float32), 0.0)
        mean_ref[...] += jnp.sum(kept, axis=1, keepdims=True)

    @pl.when(phase == 1)
    def _():
        average = mean_ref[...] / lengths.astype(jnp.float32)
        cos_low = cos_low_ref[...]
        sin_low = sin_low_ref[...]
        real_total = total_ref[:, :NB]
        imag_total = total_ref[:, NB:]
        for tile in range(TILES_PER_STEP):
            row = step * TILES_PER_STEP + tile
            cos_high = cos_high_ref[pl.ds(row, 1), :]
            sin_high = sin_high_ref[pl.ds(row, 1), :]
            cos_part = (cos_high * cos_low - sin_high * sin_low).astype(jnp.bfloat16)
            sin_part = (sin_high * cos_low + cos_high * sin_low).astype(jnp.bfloat16)
            values = raw_ref[:, tile * LANE:(tile + 1) * LANE].astype(jnp.float32)
            positions = row * LANE + lax.broadcasted_iota(jnp.int32, values.shape, 1)
            taper = taper_ref[:, pl.ds(pl.multiple_of(row * LANE, LANE), LANE)]
            samples = jnp.where(
                positions < lengths, (values - average) * taper, 0.0
            ).astype(jnp.bfloat16)
            real_total = real_total + jnp.dot(samples, cos_part, preferred_element_type=jnp.float32)
            imag_total = imag_total + jnp.dot(samples, sin_part, preferred_element_type=jnp.float32)
        total_ref[:, :NB] = real_total
        total_ref[:, NB:] = imag_total

        @pl.when(step == pl.num_programs(1) - 1)
        def _():
            groups = groups_ref[...]
            power = jnp.dot(
                real_total * real_total + imag_total * imag_total,
                groups,
                precision=lax.Precision.HIGHEST,
                preferred_element_type=jnp.float32,
            ) / SUB
            factor = lax.rsqrt(power + 1e-06)
            spread = lax.dot_general(
                factor, groups, (((1,), (1,)), ((), ())),
                precision=lax.Precision.HIGHEST,
                preferred_element_type=jnp.float32,
            )
            good = codes % 2 != 0
            real_out = (real_total * spread).astype(jnp.bfloat16)
            imag_out = (imag_total * spread).astype(jnp.bfloat16)
            zero = jnp.zeros_like(real_out)
            out_ref[:, :NB] = jnp.where(good, real_out, zero)
            out_ref[:, NB:] = jnp.where(good, imag_out, zero)


def whitened_of(raw_rows, code_rows):
    row_count = raw_rows.shape[0]
    tables = [jnp.asarray(t) for t in constant_tables()]
    block = TILES_PER_STEP * LANE
    steps = PADDED // block
    full = lambda shape: pl.BlockSpec(shape, lambda p, s: (0, 0))
    return pl.pallas_call(
        dft_kernel,
        out_shape=jax.ShapeDtypeStruct((row_count, 2 * NB), jnp.bfloat16),
        grid=(2, steps),
        in_specs=[
            pl.BlockSpec((row_count, block), lambda p, s: (0, s)),
            full((row_count, 1)),
            full((1, PADDED)),
            full(tables[1].shape),
            full(tables[1].shape),
            full(tables[2].shape),
            full(tables[2].shape),
            full(tables[5].shape),
        ],
        out_specs=full((row_count, 2 * NB)),
        scratch_shapes=[
            pltpu.VMEM((row_count, 2 * NB), jnp.float32),
            pltpu.VMEM((row_count, 1), jnp.float32),
        ],
        compiler_params=pltpu.CompilerParams(dimension_semantics=("arbitrary", "arbitrary")),
        cost_estimate=pl.CostEstimate(
            flops=2 * row_count * PADDED * 2 * NB,
            transcendentals=0,
            bytes_accessed=2 * row_count * WIN * 2 + row_count * 2 * NB * 2,
        ),
    )(raw_rows, code_rows, tables[4], tables[0], tables[1], tables[2], tables[3], tables[5])


def device_index(z, y, core):
    return z * 4 + y * 2 + core


def across(valid):
    return [
        (device_index(z, y, core), device_index(z, 1 - y, core))
        for z in range(4) if valid(z) for y in range(2) for core in range(2)
    ]


def compact(own, ups, downs, z):
    line = jnp.zeros((4,) + own.shape, own.dtype)
    for hop in (3, 2, 1):
        line = lax.dynamic_update_index_in_dim(line, ups[hop - 1], jnp.maximum(z - hop, 0), 0)
    for hop in (3, 2, 1):
        line = lax.dynamic_update_index_in_dim(line, downs[hop - 1], jnp.minimum(z + hop, 3), 0)
    return lax.dynamic_update_index_in_dim(line, own, z, 0)


def line_gather(block):
    me = lax.axis_index("chan")
    z = me // 4
    y = (me // 2) % 2
    core = me % 2
    up = [(device_index(a, b, c), device_index(a + 1, b, c)) for a in range(3) for b in range(2) for c in range(2)]
    down = [(device_index(a, b, c), device_index(a - 1, b, c)) for a in range(1, 4) for b in range(2) for c in range(2)]
    other_own = lax.ppermute(block, "chan", across(lambda a: True))
    ups, downs = [], []
    going_up = going_down = block
    for hop in range(1, 4):
        going_up = lax.ppermute(going_up, "chan", up)
        going_down = lax.ppermute(going_down, "chan", down)
        ups.append(going_up)
        downs.append(going_down)
    first = lax.ppermute(jnp.stack([ups[0], downs[0]]), "chan", across(lambda a: True))
    second = lax.ppermute(jnp.where(z >= 2, ups[1], downs[1]), "chan", across(lambda a: True))
    third = lax.ppermute(jnp.where(z == 3, ups[2], downs[2]), "chan", across(lambda a: a in (0, 3)))
    other = jnp.zeros((4,) + block.shape, block.dtype)
    other = lax.dynamic_update_index_in_dim(other, third, jnp.where(z == 3, 0, 3), 0)
    other = lax.dynamic_update_index_in_dim(other, second, jnp.where(z >= 2, z - 2, z + 2), 0)
    other = lax.dynamic_update_index_in_dim(other, first[0], jnp.maximum(z - 1, 0), 0)
    other = lax.dynamic_update_index_in_dim(other, first[1], jnp.minimum(z + 1, 3), 0)
    other = lax.dynamic_update_index_in_dim(other, other_own, z, 0)
    both = jnp.concatenate([compact(block, ups, downs, z), other], 0)
    sibling = lax.ppermute(both, "chan", [(i, i ^ 1) for i in range(16)])
    gathered = jnp.concatenate([both, sibling], 0)
    slots = jnp.arange(16, dtype=jnp.int32)
    part = slots // 4
    slot_y = jnp.where(part % 2 == 0, y, 1 - y)
    slot_core = jnp.where(part < 2, core, 1 - core)
    owner = device_index(slots % 4, slot_y, slot_core)
    return gathered.reshape((16 * block.shape[0],) + block.shape[1:]), owner


def body(use_lines, raw, lengths, quality, assignment):
    my_index = lax.axis_index("chan")
    block_rows, window_count, sample_count = raw.shape
    total_channels = assignment.shape[0]
    row_count = block_rows * window_count
    my_quality = lax.dynamic_slice_in_dim(quality, my_index * block_rows, block_rows)
    codes = lengths * 2 + (my_quality[:, None] != 0).astype(jnp.int32)
    whitened = whitened_of(
        raw.reshape(row_count, sample_count), codes.reshape(row_count, 1)
    ).reshape(block_rows, window_count, 2, NB)
    panel = lax.all_to_all(whitened, "freq", split_axis=3, concat_axis=1, tiled=True)
    all_windows = panel.shape[1]
    bins_here = panel.shape[3]
    if use_lines:
        gathered, owner = line_gather(panel)
        rows = jnp.arange(block_rows, dtype=jnp.int32)
        slot_channel = (owner[:, None] * block_rows + rows[None, :]).reshape(total_channels)
        slot_assignment = jnp.take(assignment, slot_channel)
    else:
        gathered = lax.all_gather(panel, "chan", axis=0, tiled=True)
        slot_assignment = assignment
    positions = jnp.arange(total_channels, dtype=jnp.int32)
    onehot = (slot_assignment[:, None] == positions[None, :]).astype(jnp.bfloat16)
    right = jnp.einsum(
        "cwpb,cj->bpwj", gathered, onehot, preferred_element_type=jnp.float32
    ).astype(jnp.bfloat16).reshape(bins_here, 2 * all_windows, total_channels)
    mine = my_index * block_rows + jnp.arange(block_rows, dtype=jnp.int32)
    select = (slot_assignment[:, None] == mine[None, :]).astype(jnp.bfloat16)
    rotation = jnp.array(
        [[[1.0, 0.0], [0.0, -1.0]], [[0.0, 1.0], [1.0, 0.0]]], dtype=jnp.bfloat16
    )
    spread = select[:, None, :, None, None] * rotation[None, :, None, :, :]
    left_rows = jnp.einsum(
        "cwpb,cpiqr->biqrw", gathered, spread, preferred_element_type=jnp.float32
    ).astype(jnp.bfloat16).reshape(bins_here, block_rows * 2, 2 * all_windows)
    out = jnp.einsum("bik,bkj->bij", left_rows, right, preferred_element_type=jnp.float32)
    return (out / all_windows).astype(jnp.bfloat16).reshape(bins_here, block_rows, 2, total_channels)


def lines_fit(mesh):
    if dict(mesh.shape) != {"groups": mesh.shape["groups"], "chan": 16, "freq": 1}:
        return False
    devices = mesh.devices.reshape(mesh.shape["groups"], 16)
    for group in devices:
        first = getattr(group[0], "coords", None)
        if first is None:
            return False
        for position, device in enumerate(group):
            z, y, core = position // 4, (position // 2) % 2, position % 2
            where = tuple(device.coords)
            if getattr(device, "core_on_chip", None) != core:
                return False
            if where != (first[0], first[1] + y, first[2] + z):
                return False
    return True


def solution(mesh):
    return jax.shard_map(
        functools.partial(body, lines_fit(mesh)),
        mesh=mesh,
        in_specs=(
            P(("groups", "chan"), "freq", None),
            P(("groups", "chan"), "freq"),
            P("groups"),
            P("groups"),
        ),
        out_specs=P("freq", ("groups", "chan"), None, None),
        check_vma=False,
    )
```

```python
import functools
import math

import numpy as np

import jax
import jax.numpy as jnp
from jax import lax
from jax.experimental import pallas as pl
from jax.experimental.pallas import tpu as pltpu
from jax.sharding import PartitionSpec as P

WIN = 12000
NB = 512
K0 = 6
SUB = 32
LANE = 128
PADDED = 12288
TILES_PER_STEP = 24


def small_table(sample_values):
    bin_index = K0 + np.arange(NB, dtype=np.int64)
    residue = sample_values[:, None] * bin_index[None, :] % WIN
    angles = residue.astype(np.float64) * (2.0 * math.pi / WIN)
    return np.cos(angles).astype(np.float32), (-np.sin(angles)).astype(np.float32)


def constant_tables():
    high_count = PADDED // LANE
    cos_high, sin_high = small_table(np.arange(high_count, dtype=np.int64) * LANE)
    cos_low, sin_low = small_table(np.arange(LANE, dtype=np.int64))
    positions = np.arange(PADDED, dtype=np.float64)
    taper = (0.5 - 0.5 * np.cos(positions * (2.0 * math.pi / WIN))).astype(np.float32)
    groups = (np.arange(NB)[:, None] // SUB == np.arange(NB // SUB)[None, :]).astype(np.float32)
    return cos_high, sin_high, cos_low, sin_low, taper.reshape(1, PADDED), groups


def dft_kernel(
    raw_ref, code_ref, taper_ref, cos_high_ref, sin_high_ref, cos_low_ref,
    sin_low_ref, groups_ref, out_ref, total_ref, mean_ref,
):
    phase = pl.program_id(0)
    step = pl.program_id(1)
    block = TILES_PER_STEP * LANE
    codes = code_ref[...]
    lengths = codes // 2

    @pl.when(jnp.logical_and(phase == 0, step == 0))
    def _():
        mean_ref[...] = jnp.zeros_like(mean_ref)
        total_ref[...] = jnp.zeros_like(total_ref)

    @pl.when(phase == 0)
    def _():
        positions = step * block + lax.broadcasted_iota(jnp.int32, raw_ref.shape, 1)
        inside = positions < lengths
        kept = jnp.where(inside, raw_ref[...].astype(jnp.float32), 0.0)
        mean_ref[...] += jnp.sum(kept, axis=1, keepdims=True)

    @pl.when(phase == 1)
    def _():
        average = mean_ref[...] / lengths.astype(jnp.float32)
        cos_low = cos_low_ref[...]
        sin_low = sin_low_ref[...]
        real_total = total_ref[:, :NB]
        imag_total = total_ref[:, NB:]
        for tile in range(TILES_PER_STEP):
            row = step * TILES_PER_STEP + tile
            cos_high = cos_high_ref[pl.ds(row, 1), :]
            sin_high = sin_high_ref[pl.ds(row, 1), :]
            cos_part = (cos_high * cos_low - sin_high * sin_low).astype(jnp.bfloat16)
            sin_part = (sin_high * cos_low + cos_high * sin_low).astype(jnp.bfloat16)
            values = raw_ref[:, tile * LANE:(tile + 1) * LANE].astype(jnp.float32)
            positions = row * LANE + lax.broadcasted_iota(jnp.int32, values.shape, 1)
            taper = taper_ref[:, pl.ds(pl.multiple_of(row * LANE, LANE), LANE)]
            samples = jnp.where(
                positions < lengths, (values - average) * taper, 0.0
            ).astype(jnp.bfloat16)
            real_total = real_total + jnp.dot(samples, cos_part, preferred_element_type=jnp.float32)
            imag_total = imag_total + jnp.dot(samples, sin_part, preferred_element_type=jnp.float32)
        total_ref[:, :NB] = real_total
        total_ref[:, NB:] = imag_total

        @pl.when(step == pl.num_programs(1) - 1)
        def _():
            groups = groups_ref[...]
            power = jnp.dot(
                real_total * real_total + imag_total * imag_total,
                groups,
                precision=lax.Precision.HIGHEST,
                preferred_element_type=jnp.float32,
            ) / SUB
            factor = lax.rsqrt(power + 1e-06)
            spread = lax.dot_general(
                factor, groups, (((1,), (1,)), ((), ())),
                precision=lax.Precision.HIGHEST,
                preferred_element_type=jnp.float32,
            )
            good = codes % 2 != 0
            real_out = (real_total * spread).astype(jnp.bfloat16)
            imag_out = (imag_total * spread).astype(jnp.bfloat16)
            zero = jnp.zeros_like(real_out)
            out_ref[:, :NB] = jnp.where(good, real_out, zero)
            out_ref[:, NB:] = jnp.where(good, imag_out, zero)


def whitened_of(raw_rows, code_rows):
    row_count = raw_rows.shape[0]
    tables = [jnp.asarray(t) for t in constant_tables()]
    block = TILES_PER_STEP * LANE
    steps = PADDED // block
    full = lambda shape: pl.BlockSpec(shape, lambda p, s: (0, 0))
    return pl.pallas_call(
        dft_kernel,
        out_shape=jax.ShapeDtypeStruct((row_count, 2 * NB), jnp.bfloat16),
        grid=(2, steps),
        in_specs=[
            pl.BlockSpec((row_count, block), lambda p, s: (0, s)),
            full((row_count, 1)),
            full((1, PADDED)),
            full(tables[1].shape),
            full(tables[1].shape),
            full(tables[2].shape),
            full(tables[2].shape),
            full(tables[5].shape),
        ],
        out_specs=full((row_count, 2 * NB)),
        scratch_shapes=[
            pltpu.VMEM((row_count, 2 * NB), jnp.float32),
            pltpu.VMEM((row_count, 1), jnp.float32),
        ],
        compiler_params=pltpu.CompilerParams(dimension_semantics=("arbitrary", "arbitrary")),
        cost_estimate=pl.CostEstimate(
            flops=2 * row_count * PADDED * 2 * NB,
            transcendentals=0,
            bytes_accessed=2 * row_count * WIN * 2 + row_count * 2 * NB * 2,
        ),
    )(raw_rows, code_rows, tables[4], tables[0], tables[1], tables[2], tables[3], tables[5])


def device_index(z, y, core):
    return z * 4 + y * 2 + core


def across(valid):
    return [
        (device_index(z, y, core), device_index(z, 1 - y, core))
        for z in range(4) if valid(z) for y in range(2) for core in range(2)
    ]


def compact(own, ups, downs, z):
    line = jnp.zeros((4,) + own.shape, own.dtype)
    for hop in (3, 2, 1):
        line = lax.dynamic_update_index_in_dim(line, ups[hop - 1], jnp.maximum(z - hop, 0), 0)
    for hop in (3, 2, 1):
        line = lax.dynamic_update_index_in_dim(line, downs[hop - 1], jnp.minimum(z + hop, 3), 0)
    return lax.dynamic_update_index_in_dim(line, own, z, 0)


def line_gather(block):
    me = lax.axis_index("chan")
    z = me // 4
    y = (me // 2) % 2
    core = me % 2
    def shift(distance):
        return [
            (device_index(a, b, c), device_index(a + distance, b, c))
            for a in range(4) if 0 <= a + distance < 4 for b in range(2) for c in range(2)
        ]

    other_own = lax.ppermute(block, "chan", across(lambda a: True))
    ups = [lax.ppermute(block, "chan", shift(1)), lax.ppermute(block, "chan", shift(2))]
    downs = [lax.ppermute(block, "chan", shift(-1)), lax.ppermute(block, "chan", shift(-2))]
    ups.append(lax.ppermute(ups[1], "chan", shift(1)))
    downs.append(lax.ppermute(downs[1], "chan", shift(-1)))
    first = lax.ppermute(jnp.stack([ups[0], downs[0]]), "chan", across(lambda a: True))
    second = lax.ppermute(jnp.where(z >= 2, ups[1], downs[1]), "chan", across(lambda a: True))
    third = lax.ppermute(jnp.where(z == 3, ups[2], downs[2]), "chan", across(lambda a: a in (0, 3)))
    other = jnp.zeros((4,) + block.shape, block.dtype)
    other = lax.dynamic_update_index_in_dim(other, third, jnp.where(z == 3, 0, 3), 0)
    other = lax.dynamic_update_index_in_dim(other, second, jnp.where(z >= 2, z - 2, z + 2), 0)
    other = lax.dynamic_update_index_in_dim(other, first[0], jnp.maximum(z - 1, 0), 0)
    other = lax.dynamic_update_index_in_dim(other, first[1], jnp.minimum(z + 1, 3), 0)
    other = lax.dynamic_update_index_in_dim(other, other_own, z, 0)
    both = jnp.concatenate([compact(block, ups, downs, z), other], 0)
    sibling = lax.ppermute(both, "chan", [(i, i ^ 1) for i in range(16)])
    gathered = jnp.concatenate([both, sibling], 0)
    slots = jnp.arange(16, dtype=jnp.int32)
    part = slots // 4
    slot_y = jnp.where(part % 2 == 0, y, 1 - y)
    slot_core = jnp.where(part < 2, core, 1 - core)
    owner = device_index(slots % 4, slot_y, slot_core)
    return gathered.reshape((16 * block.shape[0],) + block.shape[1:]), owner


def body(use_lines, raw, lengths, quality, assignment):
    my_index = lax.axis_index("chan")
    block_rows, window_count, sample_count = raw.shape
    total_channels = assignment.shape[0]
    row_count = block_rows * window_count
    my_quality = lax.dynamic_slice_in_dim(quality, my_index * block_rows, block_rows)
    codes = lengths * 2 + (my_quality[:, None] != 0).astype(jnp.int32)
    whitened = whitened_of(
        raw.reshape(row_count, sample_count), codes.reshape(row_count, 1)
    ).reshape(block_rows, window_count, 2, NB)
    panel = lax.all_to_all(whitened, "freq", split_axis=3, concat_axis=1, tiled=True)
    all_windows = panel.shape[1]
    bins_here = panel.shape[3]
    if use_lines:
        gathered, owner = line_gather(panel)
        rows = jnp.arange(block_rows, dtype=jnp.int32)
        slot_channel = (owner[:, None] * block_rows + rows[None, :]).reshape(total_channels)
        slot_assignment = jnp.take(assignment, slot_channel)
    else:
        gathered = lax.all_gather(panel, "chan", axis=0, tiled=True)
        slot_assignment = assignment
    positions = jnp.arange(total_channels, dtype=jnp.int32)
    onehot = (slot_assignment[:, None] == positions[None, :]).astype(jnp.bfloat16)
    right = jnp.einsum(
        "cwpb,cj->bpwj", gathered, onehot, preferred_element_type=jnp.float32
    ).astype(jnp.bfloat16).reshape(bins_here, 2 * all_windows, total_channels)
    mine = my_index * block_rows + jnp.arange(block_rows, dtype=jnp.int32)
    select = (slot_assignment[:, None] == mine[None, :]).astype(jnp.bfloat16)
    rotation = jnp.array(
        [[[1.0, 0.0], [0.0, -1.0]], [[0.0, 1.0], [1.0, 0.0]]], dtype=jnp.bfloat16
    )
    spread = select[:, None, :, None, None] * rotation[None, :, None, :, :]
    left_rows = jnp.einsum(
        "cwpb,cpiqr->biqrw", gathered, spread, preferred_element_type=jnp.float32
    ).astype(jnp.bfloat16).reshape(bins_here, block_rows * 2, 2 * all_windows)
    out = jnp.einsum("bik,bkj->bij", left_rows, right, preferred_element_type=jnp.float32)
    return (out / all_windows).astype(jnp.bfloat16).reshape(bins_here, block_rows, 2, total_channels)


def lines_fit(mesh):
    if dict(mesh.shape) != {"groups": mesh.shape["groups"], "chan": 16, "freq": 1}:
        return False
    devices = mesh.devices.reshape(mesh.shape["groups"], 16)
    for group in devices:
        first = getattr(group[0], "coords", None)
        if first is None:
            return False
        for position, device in enumerate(group):
            z, y, core = position // 4, (position // 2) % 2, position % 2
            where = tuple(device.coords)
            if getattr(device, "core_on_chip", None) != core:
                return False
            if where != (first[0], first[1] + y, first[2] + z):
                return False
    return True


def solution(mesh):
    return jax.shard_map(
        functools.partial(body, lines_fit(mesh)),
        mesh=mesh,
        in_specs=(
            P(("groups", "chan"), "freq", None),
            P(("groups", "chan"), "freq"),
            P("groups"),
            P("groups"),
        ),
        out_specs=P("freq", ("groups", "chan"), None, None),
        check_vma=False,
    )
```

```python
import functools
import math

import numpy as np

import jax
import jax.numpy as jnp
from jax import lax
from jax.experimental import pallas as pl
from jax.experimental.pallas import tpu as pltpu
from jax.sharding import PartitionSpec as P

WIN = 12000
NB = 512
K0 = 6
SUB = 32
LANE = 128
PADDED = 12288
TILES_PER_STEP = 24


def small_table(sample_values):
    bin_index = K0 + np.arange(NB, dtype=np.int64)
    residue = sample_values[:, None] * bin_index[None, :] % WIN
    angles = residue.astype(np.float64) * (2.0 * math.pi / WIN)
    return np.cos(angles).astype(np.float32), (-np.sin(angles)).astype(np.float32)


def constant_tables():
    high_count = PADDED // LANE
    cos_high, sin_high = small_table(np.arange(high_count, dtype=np.int64) * LANE)
    cos_low, sin_low = small_table(np.arange(LANE, dtype=np.int64))
    positions = np.arange(PADDED, dtype=np.float64)
    taper = (0.5 - 0.5 * np.cos(positions * (2.0 * math.pi / WIN))).astype(np.float32)
    groups = (np.arange(NB)[:, None] // SUB == np.arange(NB // SUB)[None, :]).astype(np.float32)
    return cos_high, sin_high, cos_low, sin_low, taper.reshape(1, PADDED), groups


def dft_kernel(
    raw_ref, code_ref, taper_ref, cos_high_ref, sin_high_ref, cos_low_ref,
    sin_low_ref, groups_ref, out_ref, total_ref, mean_ref,
):
    phase = pl.program_id(0)
    step = pl.program_id(1)
    block = TILES_PER_STEP * LANE
    codes = code_ref[...]
    lengths = codes // 2

    @pl.when(jnp.logical_and(phase == 0, step == 0))
    def _():
        mean_ref[...] = jnp.zeros_like(mean_ref)
        total_ref[...] = jnp.zeros_like(total_ref)

    @pl.when(phase == 0)
    def _():
        positions = step * block + lax.broadcasted_iota(jnp.int32, raw_ref.shape, 1)
        inside = positions < lengths
        kept = jnp.where(inside, raw_ref[...].astype(jnp.float32), 0.0)
        mean_ref[...] += jnp.sum(kept, axis=1, keepdims=True)

    @pl.when(phase == 1)
    def _():
        average = mean_ref[...] / lengths.astype(jnp.float32)
        cos_low = cos_low_ref[...]
        sin_low = sin_low_ref[...]
        real_total = total_ref[:, :NB]
        imag_total = total_ref[:, NB:]
        for tile in range(TILES_PER_STEP):
            row = step * TILES_PER_STEP + tile
            cos_high = cos_high_ref[pl.ds(row, 1), :]
            sin_high = sin_high_ref[pl.ds(row, 1), :]
            cos_part = (cos_high * cos_low - sin_high * sin_low).astype(jnp.bfloat16)
            sin_part = (sin_high * cos_low + cos_high * sin_low).astype(jnp.bfloat16)
            values = raw_ref[:, tile * LANE:(tile + 1) * LANE].astype(jnp.float32)
            positions = row * LANE + lax.broadcasted_iota(jnp.int32, values.shape, 1)
            taper = taper_ref[:, pl.ds(pl.multiple_of(row * LANE, LANE), LANE)]
            samples = jnp.where(
                positions < lengths, (values - average) * taper, 0.0
            ).astype(jnp.bfloat16)
            real_total = real_total + jnp.dot(samples, cos_part, preferred_element_type=jnp.float32)
            imag_total = imag_total + jnp.dot(samples, sin_part, preferred_element_type=jnp.float32)
        total_ref[:, :NB] = real_total
        total_ref[:, NB:] = imag_total

        @pl.when(step == pl.num_programs(1) - 1)
        def _():
            groups = groups_ref[...]
            power = jnp.dot(
                real_total * real_total + imag_total * imag_total,
                groups,
                precision=lax.Precision.HIGHEST,
                preferred_element_type=jnp.float32,
            ) / SUB
            factor = lax.rsqrt(power + 1e-06)
            spread = lax.dot_general(
                factor, groups, (((1,), (1,)), ((), ())),
                precision=lax.Precision.HIGHEST,
                preferred_element_type=jnp.float32,
            )
            good = codes % 2 != 0
            real_out = (real_total * spread).astype(jnp.bfloat16)
            imag_out = (imag_total * spread).astype(jnp.bfloat16)
            zero = jnp.zeros_like(real_out)
            out_ref[:, :NB] = jnp.where(good, real_out, zero)
            out_ref[:, NB:] = jnp.where(good, imag_out, zero)


def whitened_of(raw_rows, code_rows):
    row_count = raw_rows.shape[0]
    tables = [jnp.asarray(t) for t in constant_tables()]
    block = TILES_PER_STEP * LANE
    steps = PADDED // block
    full = lambda shape: pl.BlockSpec(shape, lambda p, s: (0, 0))
    return pl.pallas_call(
        dft_kernel,
        out_shape=jax.ShapeDtypeStruct((row_count, 2 * NB), jnp.bfloat16),
        grid=(2, steps),
        in_specs=[
            pl.BlockSpec((row_count, block), lambda p, s: (0, s)),
            full((row_count, 1)),
            full((1, PADDED)),
            full(tables[1].shape),
            full(tables[1].shape),
            full(tables[2].shape),
            full(tables[2].shape),
            full(tables[5].shape),
        ],
        out_specs=full((row_count, 2 * NB)),
        scratch_shapes=[
            pltpu.VMEM((row_count, 2 * NB), jnp.float32),
            pltpu.VMEM((row_count, 1), jnp.float32),
        ],
        compiler_params=pltpu.CompilerParams(dimension_semantics=("arbitrary", "arbitrary")),
        cost_estimate=pl.CostEstimate(
            flops=2 * row_count * PADDED * 2 * NB,
            transcendentals=0,
            bytes_accessed=2 * row_count * WIN * 2 + row_count * 2 * NB * 2,
        ),
    )(raw_rows, code_rows, tables[4], tables[0], tables[1], tables[2], tables[3], tables[5])


def device_index(z, y, core):
    return z * 4 + y * 2 + core


def across(valid):
    return [
        (device_index(z, y, core), device_index(z, 1 - y, core))
        for z in range(4) if valid(z) for y in range(2) for core in range(2)
    ]


def compact(own, ups, downs, z):
    line = jnp.zeros((4,) + own.shape, own.dtype)
    for hop in (3, 2, 1):
        line = lax.dynamic_update_index_in_dim(line, ups[hop - 1], jnp.maximum(z - hop, 0), 0)
    for hop in (3, 2, 1):
        line = lax.dynamic_update_index_in_dim(line, downs[hop - 1], jnp.minimum(z + hop, 3), 0)
    return lax.dynamic_update_index_in_dim(line, own, z, 0)


def line_gather(block):
    me = lax.axis_index("chan")
    z = me // 4
    y = (me // 2) % 2
    core = me % 2
    def shift(distance):
        return [
            (device_index(a, b, c), device_index(a + distance, b, c))
            for a in range(4) if 0 <= a + distance < 4 for b in range(2) for c in range(2)
        ]

    pair = jnp.stack([block, lax.ppermute(block, "chan", across(lambda a: True))])
    ups, downs = [], []
    going_up = going_down = pair
    for hop in range(3):
        going_up = lax.ppermute(going_up, "chan", shift(1))
        going_down = lax.ppermute(going_down, "chan", shift(-1))
        ups.append(going_up)
        downs.append(going_down)
    both = compact(pair, ups, downs, z)
    sibling = lax.ppermute(both, "chan", [(i, i ^ 1) for i in range(16)])
    gathered = jnp.concatenate([both, sibling], 0)
    slots = jnp.arange(16, dtype=jnp.int32)
    slot_core = jnp.where(slots < 8, core, 1 - core)
    slot_y = jnp.where(slots % 2 == 0, y, 1 - y)
    owner = device_index((slots // 2) % 4, slot_y, slot_core)
    return gathered.reshape((16 * block.shape[0],) + block.shape[1:]), owner


def body(use_lines, raw, lengths, quality, assignment):
    my_index = lax.axis_index("chan")
    block_rows, window_count, sample_count = raw.shape
    total_channels = assignment.shape[0]
    row_count = block_rows * window_count
    my_quality = lax.dynamic_slice_in_dim(quality, my_index * block_rows, block_rows)
    codes = lengths * 2 + (my_quality[:, None] != 0).astype(jnp.int32)
    whitened = whitened_of(
        raw.reshape(row_count, sample_count), codes.reshape(row_count, 1)
    ).reshape(block_rows, window_count, 2, NB)
    panel = lax.all_to_all(whitened, "freq", split_axis=3, concat_axis=1, tiled=True)
    all_windows = panel.shape[1]
    bins_here = panel.shape[3]
    if use_lines:
        gathered, owner = line_gather(panel)
        rows = jnp.arange(block_rows, dtype=jnp.int32)
        slot_channel = (owner[:, None] * block_rows + rows[None, :]).reshape(total_channels)
        slot_assignment = jnp.take(assignment, slot_channel)
    else:
        gathered = lax.all_gather(panel, "chan", axis=0, tiled=True)
        slot_assignment = assignment
    positions = jnp.arange(total_channels, dtype=jnp.int32)
    onehot = (slot_assignment[:, None] == positions[None, :]).astype(jnp.bfloat16)
    right = jnp.einsum(
        "cwpb,cj->bpwj", gathered, onehot, preferred_element_type=jnp.float32
    ).astype(jnp.bfloat16).reshape(bins_here, 2 * all_windows, total_channels)
    mine = my_index * block_rows + jnp.arange(block_rows, dtype=jnp.int32)
    select = (slot_assignment[:, None] == mine[None, :]).astype(jnp.bfloat16)
    rotation = jnp.array(
        [[[1.0, 0.0], [0.0, -1.0]], [[0.0, 1.0], [1.0, 0.0]]], dtype=jnp.bfloat16
    )
    spread = select[:, None, :, None, None] * rotation[None, :, None, :, :]
    left_rows = jnp.einsum(
        "cwpb,cpiqr->biqrw", gathered, spread, preferred_element_type=jnp.float32
    ).astype(jnp.bfloat16).reshape(bins_here, block_rows * 2, 2 * all_windows)
    out = jnp.einsum("bik,bkj->bij", left_rows, right, preferred_element_type=jnp.float32)
    return (out / all_windows).astype(jnp.bfloat16).reshape(bins_here, block_rows, 2, total_channels)


def lines_fit(mesh):
    if dict(mesh.shape) != {"groups": mesh.shape["groups"], "chan": 16, "freq": 1}:
        return False
    devices = mesh.devices.reshape(mesh.shape["groups"], 16)
    for group in devices:
        first = getattr(group[0], "coords", None)
        if first is None:
            return False
        for position, device in enumerate(group):
            z, y, core = position // 4, (position // 2) % 2, position % 2
            where = tuple(device.coords)
            if getattr(device, "core_on_chip", None) != core:
                return False
            if where != (first[0], first[1] + y, first[2] + z):
                return False
    return True


def solution(mesh):
    return jax.shard_map(
        functools.partial(body, lines_fit(mesh)),
        mesh=mesh,
        in_specs=(
            P(("groups", "chan"), "freq", None),
            P(("groups", "chan"), "freq"),
            P("groups"),
            P("groups"),
        ),
        out_specs=P("freq", ("groups", "chan"), None, None),
        check_vma=False,
    )
```

```python
import functools
import math

import numpy as np

import jax
import jax.numpy as jnp
from jax import lax
from jax.experimental import pallas as pl
from jax.experimental.pallas import tpu as pltpu
from jax.sharding import PartitionSpec as P

WIN = 12000
NB = 512
K0 = 6
SUB = 32
LANE = 128
PADDED = 12288
TILES_PER_STEP = 48


def small_table(sample_values):
    bin_index = K0 + np.arange(NB, dtype=np.int64)
    residue = sample_values[:, None] * bin_index[None, :] % WIN
    angles = residue.astype(np.float64) * (2.0 * math.pi / WIN)
    return np.cos(angles).astype(np.float32), (-np.sin(angles)).astype(np.float32)


def constant_tables():
    high_count = PADDED // LANE
    cos_high, sin_high = small_table(np.arange(high_count, dtype=np.int64) * LANE)
    cos_low, sin_low = small_table(np.arange(LANE, dtype=np.int64))
    positions = np.arange(PADDED, dtype=np.float64)
    taper = (0.5 - 0.5 * np.cos(positions * (2.0 * math.pi / WIN))).astype(np.float32)
    groups = (np.arange(NB)[:, None] // SUB == np.arange(NB // SUB)[None, :]).astype(np.float32)
    return cos_high, sin_high, cos_low, sin_low, taper.reshape(1, PADDED), groups


def dft_kernel(
    raw_ref, code_ref, taper_ref, cos_high_ref, sin_high_ref, cos_low_ref,
    sin_low_ref, groups_ref, out_ref, total_ref, mean_ref,
):
    phase = pl.program_id(0)
    step = pl.program_id(1)
    block = TILES_PER_STEP * LANE
    codes = code_ref[...]
    lengths = codes // 2

    @pl.when(jnp.logical_and(phase == 0, step == 0))
    def _():
        mean_ref[...] = jnp.zeros_like(mean_ref)
        total_ref[...] = jnp.zeros_like(total_ref)

    @pl.when(phase == 0)
    def _():
        positions = step * block + lax.broadcasted_iota(jnp.int32, raw_ref.shape, 1)
        inside = positions < lengths
        kept = jnp.where(inside, raw_ref[...].astype(jnp.float32), 0.0)
        mean_ref[...] += jnp.sum(kept, axis=1, keepdims=True)

    @pl.when(phase == 1)
    def _():
        average = mean_ref[...] / lengths.astype(jnp.float32)
        cos_low = cos_low_ref[...]
        sin_low = sin_low_ref[...]
        real_total = total_ref[:, :NB]
        imag_total = total_ref[:, NB:]
        for tile in range(TILES_PER_STEP):
            row = step * TILES_PER_STEP + tile
            cos_high = cos_high_ref[pl.ds(row, 1), :]
            sin_high = sin_high_ref[pl.ds(row, 1), :]
            cos_part = (cos_high * cos_low - sin_high * sin_low).astype(jnp.bfloat16)
            sin_part = (sin_high * cos_low + cos_high * sin_low).astype(jnp.bfloat16)
            values = raw_ref[:, tile * LANE:(tile + 1) * LANE].astype(jnp.float32)
            positions = row * LANE + lax.broadcasted_iota(jnp.int32, values.shape, 1)
            taper = taper_ref[:, pl.ds(pl.multiple_of(row * LANE, LANE), LANE)]
            samples = jnp.where(
                positions < lengths, (values - average) * taper, 0.0
            ).astype(jnp.bfloat16)
            real_total = real_total + jnp.dot(samples, cos_part, preferred_element_type=jnp.float32)
            imag_total = imag_total + jnp.dot(samples, sin_part, preferred_element_type=jnp.float32)
        total_ref[:, :NB] = real_total
        total_ref[:, NB:] = imag_total

        @pl.when(step == pl.num_programs(1) - 1)
        def _():
            groups = groups_ref[...]
            power = jnp.dot(
                real_total * real_total + imag_total * imag_total,
                groups,
                precision=lax.Precision.HIGHEST,
                preferred_element_type=jnp.float32,
            ) / SUB
            factor = lax.rsqrt(power + 1e-06)
            spread = lax.dot_general(
                factor, groups, (((1,), (1,)), ((), ())),
                precision=lax.Precision.HIGHEST,
                preferred_element_type=jnp.float32,
            )
            good = codes % 2 != 0
            real_out = (real_total * spread).astype(jnp.bfloat16)
            imag_out = (imag_total * spread).astype(jnp.bfloat16)
            zero = jnp.zeros_like(real_out)
            out_ref[:, :NB] = jnp.where(good, real_out, zero)
            out_ref[:, NB:] = jnp.where(good, imag_out, zero)


def whitened_of(raw_rows, code_rows):
    row_count = raw_rows.shape[0]
    tables = [jnp.asarray(t) for t in constant_tables()]
    block = TILES_PER_STEP * LANE
    steps = PADDED // block
    full = lambda shape: pl.BlockSpec(shape, lambda p, s: (0, 0))
    return pl.pallas_call(
        dft_kernel,
        out_shape=jax.ShapeDtypeStruct((row_count, 2 * NB), jnp.bfloat16),
        grid=(2, steps),
        in_specs=[
            pl.BlockSpec((row_count, block), lambda p, s: (0, s)),
            full((row_count, 1)),
            full((1, PADDED)),
            full(tables[1].shape),
            full(tables[1].shape),
            full(tables[2].shape),
            full(tables[2].shape),
            full(tables[5].shape),
        ],
        out_specs=full((row_count, 2 * NB)),
        scratch_shapes=[
            pltpu.VMEM((row_count, 2 * NB), jnp.float32),
            pltpu.VMEM((row_count, 1), jnp.float32),
        ],
        compiler_params=pltpu.CompilerParams(dimension_semantics=("arbitrary", "arbitrary")),
        cost_estimate=pl.CostEstimate(
            flops=2 * row_count * PADDED * 2 * NB,
            transcendentals=0,
            bytes_accessed=2 * row_count * WIN * 2 + row_count * 2 * NB * 2,
        ),
    )(raw_rows, code_rows, tables[4], tables[0], tables[1], tables[2], tables[3], tables[5])


def device_index(z, y, core):
    return z * 4 + y * 2 + core


def across(valid):
    return [
        (device_index(z, y, core), device_index(z, 1 - y, core))
        for z in range(4) if valid(z) for y in range(2) for core in range(2)
    ]


def compact(own, ups, downs, z):
    line = jnp.zeros((4,) + own.shape, own.dtype)
    for hop in (3, 2, 1):
        line = lax.dynamic_update_index_in_dim(line, ups[hop - 1], jnp.maximum(z - hop, 0), 0)
    for hop in (3, 2, 1):
        line = lax.dynamic_update_index_in_dim(line, downs[hop - 1], jnp.minimum(z + hop, 3), 0)
    return lax.dynamic_update_index_in_dim(line, own, z, 0)


def line_gather(block):
    me = lax.axis_index("chan")
    z = me // 4
    y = (me // 2) % 2
    core = me % 2
    def shift(distance):
        return [
            (device_index(a, b, c), device_index(a + distance, b, c))
            for a in range(4) if 0 <= a + distance < 4 for b in range(2) for c in range(2)
        ]

    other_own = lax.ppermute(block, "chan", across(lambda a: True))
    ups = [lax.ppermute(block, "chan", shift(1)), lax.ppermute(block, "chan", shift(2))]
    downs = [lax.ppermute(block, "chan", shift(-1)), lax.ppermute(block, "chan", shift(-2))]
    ups.append(lax.ppermute(ups[1], "chan", shift(1)))
    downs.append(lax.ppermute(downs[1], "chan", shift(-1)))
    first = lax.ppermute(jnp.stack([ups[0], downs[0]]), "chan", across(lambda a: True))
    second = lax.ppermute(jnp.where(z >= 2, ups[1], downs[1]), "chan", across(lambda a: True))
    third = lax.ppermute(jnp.where(z == 3, ups[2], downs[2]), "chan", across(lambda a: a in (0, 3)))
    other = jnp.zeros((4,) + block.shape, block.dtype)
    other = lax.dynamic_update_index_in_dim(other, third, jnp.where(z == 3, 0, 3), 0)
    other = lax.dynamic_update_index_in_dim(other, second, jnp.where(z >= 2, z - 2, z + 2), 0)
    other = lax.dynamic_update_index_in_dim(other, first[0], jnp.maximum(z - 1, 0), 0)
    other = lax.dynamic_update_index_in_dim(other, first[1], jnp.minimum(z + 1, 3), 0)
    other = lax.dynamic_update_index_in_dim(other, other_own, z, 0)
    both = jnp.concatenate([compact(block, ups, downs, z), other], 0)
    sibling = lax.ppermute(both, "chan", [(i, i ^ 1) for i in range(16)])
    gathered = jnp.concatenate([both, sibling], 0)
    slots = jnp.arange(16, dtype=jnp.int32)
    part = slots // 4
    slot_y = jnp.where(part % 2 == 0, y, 1 - y)
    slot_core = jnp.where(part < 2, core, 1 - core)
    owner = device_index(slots % 4, slot_y, slot_core)
    return gathered.reshape((16 * block.shape[0],) + block.shape[1:]), owner


def body(use_lines, raw, lengths, quality, assignment):
    my_index = lax.axis_index("chan")
    block_rows, window_count, sample_count = raw.shape
    total_channels = assignment.shape[0]
    row_count = block_rows * window_count
    my_quality = lax.dynamic_slice_in_dim(quality, my_index * block_rows, block_rows)
    codes = lengths * 2 + (my_quality[:, None] != 0).astype(jnp.int32)
    whitened = whitened_of(
        raw.reshape(row_count, sample_count), codes.reshape(row_count, 1)
    ).reshape(block_rows, window_count, 2, NB)
    panel = lax.all_to_all(whitened, "freq", split_axis=3, concat_axis=1, tiled=True)
    all_windows = panel.shape[1]
    bins_here = panel.shape[3]
    if use_lines:
        gathered, owner = line_gather(panel)
        rows = jnp.arange(block_rows, dtype=jnp.int32)
        slot_channel = (owner[:, None] * block_rows + rows[None, :]).reshape(total_channels)
        slot_assignment = jnp.take(assignment, slot_channel)
    else:
        gathered = lax.all_gather(panel, "chan", axis=0, tiled=True)
        slot_assignment = assignment
    positions = jnp.arange(total_channels, dtype=jnp.int32)
    onehot = (slot_assignment[:, None] == positions[None, :]).astype(jnp.bfloat16)
    right = gathered.transpose(3, 2, 1, 0).reshape(bins_here, 2 * all_windows, total_channels)
    mine = my_index * block_rows + jnp.arange(block_rows, dtype=jnp.int32)
    select = (slot_assignment[:, None] == mine[None, :]).astype(jnp.bfloat16)
    rotation = jnp.array(
        [[[1.0, 0.0], [0.0, -1.0]], [[0.0, 1.0], [1.0, 0.0]]], dtype=jnp.bfloat16
    )
    spread = select[:, None, :, None, None] * rotation[None, :, None, :, :]
    left_rows = jnp.einsum(
        "cwpb,cpiqr->biqrw", gathered, spread, preferred_element_type=jnp.float32
    ).astype(jnp.bfloat16).reshape(bins_here, block_rows * 2, 2 * all_windows)
    sums = jnp.einsum("bik,bkc->bic", left_rows, right, preferred_element_type=jnp.float32)
    out = jnp.einsum(
        "bic,cj->bij", sums.astype(jnp.bfloat16), onehot, preferred_element_type=jnp.float32
    )
    return (out / all_windows).astype(jnp.bfloat16).reshape(bins_here, block_rows, 2, total_channels)


def lines_fit(mesh):
    if dict(mesh.shape) != {"groups": mesh.shape["groups"], "chan": 16, "freq": 1}:
        return False
    devices = mesh.devices.reshape(mesh.shape["groups"], 16)
    for group in devices:
        first = getattr(group[0], "coords", None)
        if first is None:
            return False
        for position, device in enumerate(group):
            z, y, core = position // 4, (position // 2) % 2, position % 2
            where = tuple(device.coords)
            if getattr(device, "core_on_chip", None) != core:
                return False
            if where != (first[0], first[1] + y, first[2] + z):
                return False
    return True


def solution(mesh):
    return jax.shard_map(
        functools.partial(body, lines_fit(mesh)),
        mesh=mesh,
        in_specs=(
            P(("groups", "chan"), "freq", None),
            P(("groups", "chan"), "freq"),
            P("groups"),
            P("groups"),
        ),
        out_specs=P("freq", ("groups", "chan"), None, None),
        check_vma=False,
    )
```

```python
import functools
import math

import numpy as np

import jax
import jax.numpy as jnp
from jax import lax
from jax.experimental import pallas as pl
from jax.experimental.pallas import tpu as pltpu
from jax.sharding import PartitionSpec as P

WIN = 12000
NB = 512
K0 = 6
SUB = 32
LANE = 128
PADDED = 12288
TILES_PER_STEP = 48


def small_table(sample_values):
    bin_index = K0 + np.arange(NB, dtype=np.int64)
    residue = sample_values[:, None] * bin_index[None, :] % WIN
    angles = residue.astype(np.float64) * (2.0 * math.pi / WIN)
    return np.cos(angles).astype(np.float32), (-np.sin(angles)).astype(np.float32)


def constant_tables():
    high_count = PADDED // LANE
    cos_high, sin_high = small_table(np.arange(high_count, dtype=np.int64) * LANE)
    cos_low, sin_low = small_table(np.arange(LANE, dtype=np.int64))
    positions = np.arange(PADDED, dtype=np.float64)
    taper = (0.5 - 0.5 * np.cos(positions * (2.0 * math.pi / WIN))).astype(np.float32)
    groups = (np.arange(NB)[:, None] // SUB == np.arange(NB // SUB)[None, :]).astype(np.float32)
    return cos_high, sin_high, cos_low, sin_low, taper.reshape(1, PADDED), groups


def dft_kernel(
    raw_ref, code_ref, taper_ref, cos_high_ref, sin_high_ref, cos_low_ref,
    sin_low_ref, groups_ref, out_ref, total_ref, mean_ref,
):
    phase = pl.program_id(0)
    step = pl.program_id(1)
    block = TILES_PER_STEP * LANE
    codes = code_ref[...]
    lengths = codes // 2

    @pl.when(jnp.logical_and(phase == 0, step == 0))
    def _():
        mean_ref[...] = jnp.zeros_like(mean_ref)
        total_ref[...] = jnp.zeros_like(total_ref)

    @pl.when(phase == 0)
    def _():
        positions = step * block + lax.broadcasted_iota(jnp.int32, raw_ref.shape, 1)
        inside = positions < lengths
        kept = jnp.where(inside, raw_ref[...].astype(jnp.float32), 0.0)
        mean_ref[...] += jnp.sum(kept, axis=1, keepdims=True)

    @pl.when(phase == 1)
    def _():
        average = mean_ref[...] / lengths.astype(jnp.float32)
        cos_low = cos_low_ref[...]
        sin_low = sin_low_ref[...]
        real_total = total_ref[:, :NB]
        imag_total = total_ref[:, NB:]
        for tile in range(TILES_PER_STEP):
            row = step * TILES_PER_STEP + tile
            cos_high = cos_high_ref[pl.ds(row, 1), :]
            sin_high = sin_high_ref[pl.ds(row, 1), :]
            cos_part = (cos_high * cos_low - sin_high * sin_low).astype(jnp.bfloat16)
            sin_part = (sin_high * cos_low + cos_high * sin_low).astype(jnp.bfloat16)
            values = raw_ref[:, tile * LANE:(tile + 1) * LANE].astype(jnp.float32)
            positions = row * LANE + lax.broadcasted_iota(jnp.int32, values.shape, 1)
            taper = taper_ref[:, pl.ds(pl.multiple_of(row * LANE, LANE), LANE)]
            samples = jnp.where(
                positions < lengths, (values - average) * taper, 0.0
            ).astype(jnp.bfloat16)
            real_total = real_total + jnp.dot(samples, cos_part, preferred_element_type=jnp.float32)
            imag_total = imag_total + jnp.dot(samples, sin_part, preferred_element_type=jnp.float32)
        total_ref[:, :NB] = real_total
        total_ref[:, NB:] = imag_total

        @pl.when(step == pl.num_programs(1) - 1)
        def _():
            groups = groups_ref[...]
            power = jnp.dot(
                real_total * real_total + imag_total * imag_total,
                groups,
                precision=lax.Precision.HIGHEST,
                preferred_element_type=jnp.float32,
            ) / SUB
            factor = lax.rsqrt(power + 1e-06)
            spread = lax.dot_general(
                factor, groups, (((1,), (1,)), ((), ())),
                precision=lax.Precision.HIGHEST,
                preferred_element_type=jnp.float32,
            )
            good = codes % 2 != 0
            real_out = (real_total * spread).astype(jnp.bfloat16)
            imag_out = (imag_total * spread).astype(jnp.bfloat16)
            zero = jnp.zeros_like(real_out)
            out_ref[:, :NB] = jnp.where(good, real_out, zero)
            out_ref[:, NB:] = jnp.where(good, imag_out, zero)


def whitened_of(raw_rows, code_rows):
    row_count = raw_rows.shape[0]
    tables = [jnp.asarray(t) for t in constant_tables()]
    block = TILES_PER_STEP * LANE
    steps = PADDED // block
    full = lambda shape: pl.BlockSpec(shape, lambda p, s: (0, 0))
    return pl.pallas_call(
        dft_kernel,
        out_shape=jax.ShapeDtypeStruct((row_count, 2 * NB), jnp.bfloat16),
        grid=(2, steps),
        in_specs=[
            pl.BlockSpec((row_count, block), lambda p, s: (0, s)),
            full((row_count, 1)),
            full((1, PADDED)),
            full(tables[1].shape),
            full(tables[1].shape),
            full(tables[2].shape),
            full(tables[2].shape),
            full(tables[5].shape),
        ],
        out_specs=full((row_count, 2 * NB)),
        scratch_shapes=[
            pltpu.VMEM((row_count, 2 * NB), jnp.float32),
            pltpu.VMEM((row_count, 1), jnp.float32),
        ],
        compiler_params=pltpu.CompilerParams(dimension_semantics=("arbitrary", "arbitrary")),
        cost_estimate=pl.CostEstimate(
            flops=2 * row_count * PADDED * 2 * NB,
            transcendentals=0,
            bytes_accessed=2 * row_count * WIN * 2 + row_count * 2 * NB * 2,
        ),
    )(raw_rows, code_rows, tables[4], tables[0], tables[1], tables[2], tables[3], tables[5])


def device_index(z, y, core):
    return z * 4 + y * 2 + core


def across(valid):
    return [
        (device_index(z, y, core), device_index(z, 1 - y, core))
        for z in range(4) if valid(z) for y in range(2) for core in range(2)
    ]


def compact(own, ups, downs, z):
    line = jnp.zeros((4,) + own.shape, own.dtype)
    for hop in (3, 2, 1):
        line = lax.dynamic_update_index_in_dim(line, ups[hop - 1], jnp.maximum(z - hop, 0), 0)
    for hop in (3, 2, 1):
        line = lax.dynamic_update_index_in_dim(line, downs[hop - 1], jnp.minimum(z + hop, 3), 0)
    return lax.dynamic_update_index_in_dim(line, own, z, 0)


def line_gather(block):
    me = lax.axis_index("chan")
    z = me // 4
    y = (me // 2) % 2
    core = me % 2
    def shift(distance):
        return [
            (device_index(a, b, c), device_index(a + distance, b, c))
            for a in range(4) if 0 <= a + distance < 4 for b in range(2) for c in range(2)
        ]

    other_own = lax.ppermute(block, "chan", across(lambda a: True))
    ups = [lax.ppermute(block, "chan", shift(1)), lax.ppermute(block, "chan", shift(2))]
    downs = [lax.ppermute(block, "chan", shift(-1)), lax.ppermute(block, "chan", shift(-2))]
    ups.append(lax.ppermute(ups[1], "chan", shift(1)))
    downs.append(lax.ppermute(downs[1], "chan", shift(-1)))
    first = lax.ppermute(jnp.stack([ups[0], downs[0]]), "chan", across(lambda a: True))
    second = lax.ppermute(jnp.where(z >= 2, ups[1], downs[1]), "chan", across(lambda a: True))
    third = lax.ppermute(jnp.where(z == 3, ups[2], downs[2]), "chan", across(lambda a: a in (0, 3)))
    other = jnp.zeros((4,) + block.shape, block.dtype)
    other = lax.dynamic_update_index_in_dim(other, third, jnp.where(z == 3, 0, 3), 0)
    other = lax.dynamic_update_index_in_dim(other, second, jnp.where(z >= 2, z - 2, z + 2), 0)
    other = lax.dynamic_update_index_in_dim(other, first[0], jnp.maximum(z - 1, 0), 0)
    other = lax.dynamic_update_index_in_dim(other, first[1], jnp.minimum(z + 1, 3), 0)
    other = lax.dynamic_update_index_in_dim(other, other_own, z, 0)
    both = jnp.concatenate([compact(block, ups, downs, z), other], 0)
    sibling = lax.ppermute(both, "chan", [(i, i ^ 1) for i in range(16)])
    gathered = jnp.concatenate([both, sibling], 0)
    slots = jnp.arange(16, dtype=jnp.int32)
    part = slots // 4
    slot_y = jnp.where(part % 2 == 0, y, 1 - y)
    slot_core = jnp.where(part < 2, core, 1 - core)
    owner = device_index(slots % 4, slot_y, slot_core)
    return gathered.reshape((16 * block.shape[0],) + block.shape[1:]), owner


def body(use_lines, raw, lengths, quality, assignment):
    my_index = lax.axis_index("chan")
    block_rows, window_count, sample_count = raw.shape
    total_channels = assignment.shape[0]
    row_count = block_rows * window_count
    my_quality = lax.dynamic_slice_in_dim(quality, my_index * block_rows, block_rows)
    codes = lengths * 2 + (my_quality[:, None] != 0).astype(jnp.int32)
    whitened = whitened_of(
        raw.reshape(row_count, sample_count), codes.reshape(row_count, 1)
    ).reshape(block_rows, window_count, 2, NB)
    panel = lax.all_to_all(whitened, "freq", split_axis=3, concat_axis=1, tiled=True)
    all_windows = panel.shape[1]
    bins_here = panel.shape[3]
    if use_lines:
        gathered, owner = line_gather(panel)
        rows = jnp.arange(block_rows, dtype=jnp.int32)
        slot_channel = (owner[:, None] * block_rows + rows[None, :]).reshape(total_channels)
        slot_assignment = jnp.take(assignment, slot_channel)
    else:
        gathered = lax.all_gather(panel, "chan", axis=0, tiled=True)
        slot_assignment = assignment
    positions = jnp.arange(total_channels, dtype=jnp.int32)
    onehot = (slot_assignment[:, None] == positions[None, :]).astype(jnp.bfloat16)
    right = jnp.einsum(
        "cwpb,cj->bpwj", gathered, onehot, preferred_element_type=jnp.float32
    ).astype(jnp.bfloat16).reshape(bins_here, 2 * all_windows, total_channels)
    mine = my_index * block_rows + jnp.arange(block_rows, dtype=jnp.int32)
    select = (slot_assignment[:, None] == mine[None, :]).astype(jnp.bfloat16)
    rotation = jnp.array(
        [[[1.0, 0.0], [0.0, -1.0]], [[0.0, 1.0], [1.0, 0.0]]], dtype=jnp.bfloat16
    )
    spread = select[:, None, :, None, None] * rotation[None, :, None, :, :]
    left_rows = jnp.einsum(
        "cwpb,cpiqr->biqrw", gathered, spread, preferred_element_type=jnp.float32
    ).astype(jnp.bfloat16).reshape(bins_here, block_rows * 2, 2 * all_windows)
    out = jnp.einsum("bik,bkj->bij", left_rows, right, preferred_element_type=jnp.float32)
    return (out / all_windows).astype(jnp.bfloat16).reshape(bins_here, block_rows, 2, total_channels)


def lines_fit(mesh):
    if dict(mesh.shape) != {"groups": mesh.shape["groups"], "chan": 16, "freq": 1}:
        return False
    devices = mesh.devices.reshape(mesh.shape["groups"], 16)
    for group in devices:
        first = getattr(group[0], "coords", None)
        if first is None:
            return False
        for position, device in enumerate(group):
            z, y, core = position // 4, (position // 2) % 2, position % 2
            where = tuple(device.coords)
            if getattr(device, "core_on_chip", None) != core:
                return False
            if where != (first[0], first[1] + y, first[2] + z):
                return False
    return True


def solution(mesh):
    return jax.shard_map(
        functools.partial(body, lines_fit(mesh)),
        mesh=mesh,
        in_specs=(
            P(("groups", "chan"), "freq", None),
            P(("groups", "chan"), "freq"),
            P("groups"),
            P("groups"),
        ),
        out_specs=P("freq", ("groups", "chan"), None, None),
        check_vma=False,
    )
```

```python
import functools
import math

import numpy as np

import jax
import jax.numpy as jnp
from jax import lax
from jax.experimental import pallas as pl
from jax.experimental.pallas import tpu as pltpu
from jax.sharding import PartitionSpec as P

WIN = 12000
NB = 512
K0 = 6
SUB = 32
LANE = 128
PADDED = 12288
TILES_PER_STEP = 48


def small_table(sample_values):
    bin_index = K0 + np.arange(NB, dtype=np.int64)
    residue = sample_values[:, None] * bin_index[None, :] % WIN
    angles = residue.astype(np.float64) * (2.0 * math.pi / WIN)
    return np.cos(angles).astype(np.float32), (-np.sin(angles)).astype(np.float32)


def constant_tables():
    high_count = PADDED // LANE
    cos_high, sin_high = small_table(np.arange(high_count, dtype=np.int64) * LANE)
    cos_low, sin_low = small_table(np.arange(LANE, dtype=np.int64))
    positions = np.arange(PADDED, dtype=np.float64)
    taper = (0.5 - 0.5 * np.cos(positions * (2.0 * math.pi / WIN))).astype(np.float32)
    groups = (np.arange(NB)[:, None] // SUB == np.arange(NB // SUB)[None, :]).astype(np.float32)
    return cos_high, sin_high, cos_low, sin_low, taper.reshape(1, PADDED), groups


def dft_kernel(
    raw_ref, code_ref, taper_ref, cos_high_ref, sin_high_ref, cos_low_ref,
    sin_low_ref, groups_ref, out_ref, total_ref, mean_ref,
):
    phase = pl.program_id(0)
    step = pl.program_id(1)
    block = TILES_PER_STEP * LANE
    lengths = code_ref[...]

    @pl.when(jnp.logical_and(phase == 0, step == 0))
    def _():
        mean_ref[...] = jnp.zeros_like(mean_ref)
        total_ref[...] = jnp.zeros_like(total_ref)

    @pl.when(phase == 0)
    def _():
        positions = step * block + lax.broadcasted_iota(jnp.int32, raw_ref.shape, 1)
        inside = positions < lengths
        kept = jnp.where(inside, raw_ref[...].astype(jnp.float32), 0.0)
        mean_ref[...] += jnp.sum(kept, axis=1, keepdims=True)

    @pl.when(phase == 1)
    def _():
        average = mean_ref[...] / lengths.astype(jnp.float32)
        cos_low = cos_low_ref[...]
        sin_low = sin_low_ref[...]
        real_total = total_ref[:, :NB]
        imag_total = total_ref[:, NB:]
        for tile in range(TILES_PER_STEP):
            row = step * TILES_PER_STEP + tile
            cos_high = cos_high_ref[pl.ds(row, 1), :]
            sin_high = sin_high_ref[pl.ds(row, 1), :]
            cos_part = (cos_high * cos_low - sin_high * sin_low).astype(jnp.bfloat16)
            sin_part = (sin_high * cos_low + cos_high * sin_low).astype(jnp.bfloat16)
            values = raw_ref[:, tile * LANE:(tile + 1) * LANE].astype(jnp.float32)
            positions = row * LANE + lax.broadcasted_iota(jnp.int32, values.shape, 1)
            taper = taper_ref[:, pl.ds(pl.multiple_of(row * LANE, LANE), LANE)]
            samples = jnp.where(
                positions < lengths, (values - average) * taper, 0.0
            ).astype(jnp.bfloat16)
            real_total = real_total + jnp.dot(samples, cos_part, preferred_element_type=jnp.float32)
            imag_total = imag_total + jnp.dot(samples, sin_part, preferred_element_type=jnp.float32)
        total_ref[:, :NB] = real_total
        total_ref[:, NB:] = imag_total

        @pl.when(step == pl.num_programs(1) - 1)
        def _():
            groups = groups_ref[...]
            power = jnp.dot(
                real_total * real_total + imag_total * imag_total,
                groups,
                precision=lax.Precision.HIGHEST,
                preferred_element_type=jnp.float32,
            ) / SUB
            factor = lax.rsqrt(power + 1e-06)
            spread = lax.dot_general(
                factor, groups, (((1,), (1,)), ((), ())),
                precision=lax.Precision.HIGHEST,
                preferred_element_type=jnp.float32,
            )
            out_ref[:, :NB] = (real_total * spread).astype(jnp.bfloat16)
            out_ref[:, NB:] = (imag_total * spread).astype(jnp.bfloat16)


def whitened_of(raw_rows, code_rows):
    row_count = raw_rows.shape[0]
    tables = [jnp.asarray(t) for t in constant_tables()]
    block = TILES_PER_STEP * LANE
    steps = PADDED // block
    full = lambda shape: pl.BlockSpec(shape, lambda p, s: (0, 0))
    return pl.pallas_call(
        dft_kernel,
        out_shape=jax.ShapeDtypeStruct((row_count, 2 * NB), jnp.bfloat16),
        grid=(2, steps),
        in_specs=[
            pl.BlockSpec((row_count, block), lambda p, s: (0, s)),
            full((row_count, 1)),
            full((1, PADDED)),
            full(tables[1].shape),
            full(tables[1].shape),
            full(tables[2].shape),
            full(tables[2].shape),
            full(tables[5].shape),
        ],
        out_specs=full((row_count, 2 * NB)),
        scratch_shapes=[
            pltpu.VMEM((row_count, 2 * NB), jnp.float32),
            pltpu.VMEM((row_count, 1), jnp.float32),
        ],
        compiler_params=pltpu.CompilerParams(dimension_semantics=("arbitrary", "arbitrary")),
        cost_estimate=pl.CostEstimate(
            flops=2 * row_count * PADDED * 2 * NB,
            transcendentals=0,
            bytes_accessed=2 * row_count * WIN * 2 + row_count * 2 * NB * 2,
        ),
    )(raw_rows, code_rows, tables[4], tables[0], tables[1], tables[2], tables[3], tables[5])


def device_index(z, y, core):
    return z * 4 + y * 2 + core


def across(valid):
    return [
        (device_index(z, y, core), device_index(z, 1 - y, core))
        for z in range(4) if valid(z) for y in range(2) for core in range(2)
    ]


def compact(own, ups, downs, z):
    line = jnp.zeros((4,) + own.shape, own.dtype)
    for hop in (3, 2, 1):
        line = lax.dynamic_update_index_in_dim(line, ups[hop - 1], jnp.maximum(z - hop, 0), 0)
    for hop in (3, 2, 1):
        line = lax.dynamic_update_index_in_dim(line, downs[hop - 1], jnp.minimum(z + hop, 3), 0)
    return lax.dynamic_update_index_in_dim(line, own, z, 0)


def line_gather(block):
    me = lax.axis_index("chan")
    z = me // 4
    y = (me // 2) % 2
    core = me % 2
    def shift(distance):
        return [
            (device_index(a, b, c), device_index(a + distance, b, c))
            for a in range(4) if 0 <= a + distance < 4 for b in range(2) for c in range(2)
        ]

    other_own = lax.ppermute(block, "chan", across(lambda a: True))
    ups = [lax.ppermute(block, "chan", shift(1)), lax.ppermute(block, "chan", shift(2))]
    downs = [lax.ppermute(block, "chan", shift(-1)), lax.ppermute(block, "chan", shift(-2))]
    ups.append(lax.ppermute(ups[1], "chan", shift(1)))
    downs.append(lax.ppermute(downs[1], "chan", shift(-1)))
    first = lax.ppermute(jnp.stack([ups[0], downs[0]]), "chan", across(lambda a: True))
    second = lax.ppermute(jnp.where(z >= 2, ups[1], downs[1]), "chan", across(lambda a: True))
    third = lax.ppermute(jnp.where(z == 3, ups[2], downs[2]), "chan", across(lambda a: a in (0, 3)))
    other = jnp.zeros((4,) + block.shape, block.dtype)
    other = lax.dynamic_update_index_in_dim(other, third, jnp.where(z == 3, 0, 3), 0)
    other = lax.dynamic_update_index_in_dim(other, second, jnp.where(z >= 2, z - 2, z + 2), 0)
    other = lax.dynamic_update_index_in_dim(other, first[0], jnp.maximum(z - 1, 0), 0)
    other = lax.dynamic_update_index_in_dim(other, first[1], jnp.minimum(z + 1, 3), 0)
    other = lax.dynamic_update_index_in_dim(other, other_own, z, 0)
    both = jnp.concatenate([compact(block, ups, downs, z), other], 0)
    sibling = lax.ppermute(both, "chan", [(i, i ^ 1) for i in range(16)])
    gathered = jnp.concatenate([both, sibling], 0)
    slots = jnp.arange(16, dtype=jnp.int32)
    part = slots // 4
    slot_y = jnp.where(part % 2 == 0, y, 1 - y)
    slot_core = jnp.where(part < 2, core, 1 - core)
    owner = device_index(slots % 4, slot_y, slot_core)
    return gathered.reshape((16 * block.shape[0],) + block.shape[1:]), owner


def body(use_lines, raw, lengths, quality, assignment):
    my_index = lax.axis_index("chan")
    block_rows, window_count, sample_count = raw.shape
    total_channels = assignment.shape[0]
    row_count = block_rows * window_count
    whitened = whitened_of(
        raw.reshape(row_count, sample_count), lengths.reshape(row_count, 1)
    ).reshape(block_rows, window_count, 2, NB)
    panel = lax.all_to_all(whitened, "freq", split_axis=3, concat_axis=1, tiled=True)
    all_windows = panel.shape[1]
    bins_here = panel.shape[3]
    if use_lines:
        gathered, owner = line_gather(panel)
        rows = jnp.arange(block_rows, dtype=jnp.int32)
        slot_channel = (owner[:, None] * block_rows + rows[None, :]).reshape(total_channels)
        slot_assignment = jnp.take(assignment, slot_channel)
        slot_quality = jnp.take(quality, slot_channel)
    else:
        gathered = lax.all_gather(panel, "chan", axis=0, tiled=True)
        slot_assignment = assignment
        slot_quality = quality
    good = (slot_quality != 0)[:, None]
    positions = jnp.arange(total_channels, dtype=jnp.int32)
    onehot = jnp.logical_and(slot_assignment[:, None] == positions[None, :], good).astype(jnp.bfloat16)
    right = jnp.einsum(
        "cwpb,cj->bpwj", gathered, onehot, preferred_element_type=jnp.float32
    ).astype(jnp.bfloat16).reshape(bins_here, 2 * all_windows, total_channels)
    mine = my_index * block_rows + jnp.arange(block_rows, dtype=jnp.int32)
    select = jnp.logical_and(slot_assignment[:, None] == mine[None, :], good).astype(jnp.bfloat16)
    rotation = jnp.array(
        [[[1.0, 0.0], [0.0, -1.0]], [[0.0, 1.0], [1.0, 0.0]]], dtype=jnp.bfloat16
    )
    spread = select[:, None, :, None, None] * rotation[None, :, None, :, :]
    left_rows = jnp.einsum(
        "cwpb,cpiqr->biqrw", gathered, spread, preferred_element_type=jnp.float32
    ).astype(jnp.bfloat16).reshape(bins_here, block_rows * 2, 2 * all_windows)
    out = jnp.einsum("bik,bkj->bij", left_rows, right, preferred_element_type=jnp.float32)
    return (out / all_windows).astype(jnp.bfloat16).reshape(bins_here, block_rows, 2, total_channels)


def lines_fit(mesh):
    if dict(mesh.shape) != {"groups": mesh.shape["groups"], "chan": 16, "freq": 1}:
        return False
    devices = mesh.devices.reshape(mesh.shape["groups"], 16)
    for group in devices:
        first = getattr(group[0], "coords", None)
        if first is None:
            return False
        for position, device in enumerate(group):
            z, y, core = position // 4, (position // 2) % 2, position % 2
            where = tuple(device.coords)
            if getattr(device, "core_on_chip", None) != core:
                return False
            if where != (first[0], first[1] + y, first[2] + z):
                return False
    return True


def solution(mesh):
    return jax.shard_map(
        functools.partial(body, lines_fit(mesh)),
        mesh=mesh,
        in_specs=(
            P(("groups", "chan"), "freq", None),
            P(("groups", "chan"), "freq"),
            P("groups"),
            P("groups"),
        ),
        out_specs=P("freq", ("groups", "chan"), None, None),
        check_vma=False,
    )
```

```python
import functools
import math

import numpy as np

import jax
import jax.numpy as jnp
from jax import lax
from jax.experimental import pallas as pl
from jax.experimental.pallas import tpu as pltpu
from jax.sharding import PartitionSpec as P

WIN = 12000
NB = 512
K0 = 6
SUB = 32
LANE = 128
PADDED = 12288
TILES_PER_STEP = 48


def small_table(sample_values):
    bin_index = K0 + np.arange(NB, dtype=np.int64)
    residue = sample_values[:, None] * bin_index[None, :] % WIN
    angles = residue.astype(np.float64) * (2.0 * math.pi / WIN)
    return np.cos(angles).astype(np.float32), (-np.sin(angles)).astype(np.float32)


def constant_tables():
    high_count = PADDED // LANE
    cos_high, sin_high = small_table(np.arange(high_count, dtype=np.int64) * LANE)
    cos_low, sin_low = small_table(np.arange(LANE, dtype=np.int64))
    positions = np.arange(PADDED, dtype=np.float64)
    taper = (0.5 - 0.5 * np.cos(positions * (2.0 * math.pi / WIN))).astype(np.float32)
    groups = (np.arange(NB)[:, None] // SUB == np.arange(NB // SUB)[None, :]).astype(np.float32)
    return cos_high, sin_high, cos_low, sin_low, taper.reshape(1, PADDED), groups


def dft_kernel(
    raw_ref, code_ref, taper_ref, cos_high_ref, sin_high_ref, cos_low_ref,
    sin_low_ref, groups_ref, out_ref, total_ref, mean_ref,
):
    phase = pl.program_id(0)
    step = pl.program_id(1)
    block = TILES_PER_STEP * LANE
    lengths = code_ref[...]

    @pl.when(jnp.logical_and(phase == 0, step == 0))
    def _():
        mean_ref[...] = jnp.zeros_like(mean_ref)
        total_ref[...] = jnp.zeros_like(total_ref)

    @pl.when(phase == 0)
    def _():
        positions = step * block + lax.broadcasted_iota(jnp.int32, raw_ref.shape, 1)
        inside = positions < lengths
        kept = jnp.where(inside, raw_ref[...].astype(jnp.float32), 0.0)
        mean_ref[...] += jnp.sum(kept, axis=1, keepdims=True)

    @pl.when(phase == 1)
    def _():
        average = mean_ref[...] / lengths.astype(jnp.float32)
        cos_low = cos_low_ref[...]
        sin_low = sin_low_ref[...]
        real_total = total_ref[:, :NB]
        imag_total = total_ref[:, NB:]
        for tile in range(TILES_PER_STEP):
            row = step * TILES_PER_STEP + tile
            cos_high = cos_high_ref[pl.ds(row, 1), :]
            sin_high = sin_high_ref[pl.ds(row, 1), :]
            cos_part = (cos_high * cos_low - sin_high * sin_low).astype(jnp.bfloat16)
            sin_part = (sin_high * cos_low + cos_high * sin_low).astype(jnp.bfloat16)
            values = raw_ref[:, tile * LANE:(tile + 1) * LANE].astype(jnp.float32)
            positions = row * LANE + lax.broadcasted_iota(jnp.int32, values.shape, 1)
            taper = taper_ref[:, pl.ds(pl.multiple_of(row * LANE, LANE), LANE)]
            samples = jnp.where(
                positions < lengths, (values - average) * taper, 0.0
            ).astype(jnp.bfloat16)
            real_total = real_total + jnp.dot(samples, cos_part, preferred_element_type=jnp.float32)
            imag_total = imag_total + jnp.dot(samples, sin_part, preferred_element_type=jnp.float32)
        total_ref[:, :NB] = real_total
        total_ref[:, NB:] = imag_total

        @pl.when(step == pl.num_programs(1) - 1)
        def _():
            groups = groups_ref[...]
            power = jnp.dot(
                real_total * real_total + imag_total * imag_total,
                groups,
                precision=lax.Precision.HIGHEST,
                preferred_element_type=jnp.float32,
            ) / SUB
            factor = lax.rsqrt(power + 1e-06)
            spread = lax.dot_general(
                factor, groups, (((1,), (1,)), ((), ())),
                precision=lax.Precision.HIGHEST,
                preferred_element_type=jnp.float32,
            )
            out_ref[:, :NB] = (real_total * spread).astype(jnp.bfloat16)
            out_ref[:, NB:] = (imag_total * spread).astype(jnp.bfloat16)


def whitened_of(raw_rows, code_rows):
    row_count = raw_rows.shape[0]
    tables = [jnp.asarray(t) for t in constant_tables()]
    block = TILES_PER_STEP * LANE
    steps = PADDED // block
    full = lambda shape: pl.BlockSpec(shape, lambda p, s: (0, 0))
    return pl.pallas_call(
        dft_kernel,
        out_shape=jax.ShapeDtypeStruct((row_count, 2 * NB), jnp.bfloat16),
        grid=(2, steps),
        in_specs=[
            pl.BlockSpec((row_count, block), lambda p, s: (0, s)),
            full((row_count, 1)),
            full((1, PADDED)),
            full(tables[1].shape),
            full(tables[1].shape),
            full(tables[2].shape),
            full(tables[2].shape),
            full(tables[5].shape),
        ],
        out_specs=full((row_count, 2 * NB)),
        scratch_shapes=[
            pltpu.VMEM((row_count, 2 * NB), jnp.float32),
            pltpu.VMEM((row_count, 1), jnp.float32),
        ],
        compiler_params=pltpu.CompilerParams(dimension_semantics=("arbitrary", "arbitrary")),
        cost_estimate=pl.CostEstimate(
            flops=2 * row_count * PADDED * 2 * NB,
            transcendentals=0,
            bytes_accessed=2 * row_count * WIN * 2 + row_count * 2 * NB * 2,
        ),
    )(raw_rows, code_rows, tables[4], tables[0], tables[1], tables[2], tables[3], tables[5])


def device_index(z, y, core):
    return z * 4 + y * 2 + core


def across(valid):
    return [
        (device_index(z, y, core), device_index(z, 1 - y, core))
        for z in range(4) if valid(z) for y in range(2) for core in range(2)
    ]


def compact(own, ups, downs, z):
    line = jnp.zeros((4,) + own.shape, own.dtype)
    for hop in (3, 2, 1):
        line = lax.dynamic_update_index_in_dim(line, ups[hop - 1], jnp.maximum(z - hop, 0), 0)
    for hop in (3, 2, 1):
        line = lax.dynamic_update_index_in_dim(line, downs[hop - 1], jnp.minimum(z + hop, 3), 0)
    return lax.dynamic_update_index_in_dim(line, own, z, 0)


def line_gather(block):
    me = lax.axis_index("chan")
    z = me // 4
    y = (me // 2) % 2
    core = me % 2
    def shift(distance):
        return [
            (device_index(a, b, c), device_index(a + distance, b, c))
            for a in range(4) if 0 <= a + distance < 4 for b in range(2) for c in range(2)
        ]

    other_own = lax.ppermute(block, "chan", across(lambda a: True))
    ups = [lax.ppermute(block, "chan", shift(1)), lax.ppermute(block, "chan", shift(2))]
    downs = [lax.ppermute(block, "chan", shift(-1)), lax.ppermute(block, "chan", shift(-2))]
    ups.append(lax.ppermute(ups[1], "chan", shift(1)))
    downs.append(lax.ppermute(downs[1], "chan", shift(-1)))
    nearby = jnp.stack([ups[0], downs[0], jnp.where(z >= 2, ups[1], downs[1])])
    first = lax.ppermute(nearby, "chan", across(lambda a: True))
    second = first[2]
    third = lax.ppermute(jnp.where(z == 3, ups[2], downs[2]), "chan", across(lambda a: a in (0, 3)))
    other = jnp.zeros((4,) + block.shape, block.dtype)
    other = lax.dynamic_update_index_in_dim(other, third, jnp.where(z == 3, 0, 3), 0)
    other = lax.dynamic_update_index_in_dim(other, second, jnp.where(z >= 2, z - 2, z + 2), 0)
    other = lax.dynamic_update_index_in_dim(other, first[0], jnp.maximum(z - 1, 0), 0)
    other = lax.dynamic_update_index_in_dim(other, first[1], jnp.minimum(z + 1, 3), 0)
    other = lax.dynamic_update_index_in_dim(other, other_own, z, 0)
    both = jnp.concatenate([compact(block, ups, downs, z), other], 0)
    sibling = lax.ppermute(both, "chan", [(i, i ^ 1) for i in range(16)])
    gathered = jnp.concatenate([both, sibling], 0)
    slots = jnp.arange(16, dtype=jnp.int32)
    part = slots // 4
    slot_y = jnp.where(part % 2 == 0, y, 1 - y)
    slot_core = jnp.where(part < 2, core, 1 - core)
    owner = device_index(slots % 4, slot_y, slot_core)
    return gathered.reshape((16 * block.shape[0],) + block.shape[1:]), owner


def body(use_lines, raw, lengths, quality, assignment):
    my_index = lax.axis_index("chan")
    block_rows, window_count, sample_count = raw.shape
    total_channels = assignment.shape[0]
    row_count = block_rows * window_count
    whitened = whitened_of(
        raw.reshape(row_count, sample_count), lengths.reshape(row_count, 1)
    ).reshape(block_rows, window_count, 2, NB)
    panel = lax.all_to_all(whitened, "freq", split_axis=3, concat_axis=1, tiled=True)
    all_windows = panel.shape[1]
    bins_here = panel.shape[3]
    if use_lines:
        gathered, owner = line_gather(panel)
        rows = jnp.arange(block_rows, dtype=jnp.int32)
        slot_channel = (owner[:, None] * block_rows + rows[None, :]).reshape(total_channels)
        slot_assignment = jnp.take(assignment, slot_channel)
        slot_quality = jnp.take(quality, slot_channel)
    else:
        gathered = lax.all_gather(panel, "chan", axis=0, tiled=True)
        slot_assignment = assignment
        slot_quality = quality
    good = (slot_quality != 0)[:, None]
    positions = jnp.arange(total_channels, dtype=jnp.int32)
    onehot = jnp.logical_and(slot_assignment[:, None] == positions[None, :], good).astype(jnp.bfloat16)
    right = jnp.einsum(
        "cwpb,cj->bpwj", gathered, onehot, preferred_element_type=jnp.float32
    ).astype(jnp.bfloat16).reshape(bins_here, 2 * all_windows, total_channels)
    mine = my_index * block_rows + jnp.arange(block_rows, dtype=jnp.int32)
    select = jnp.logical_and(slot_assignment[:, None] == mine[None, :], good).astype(jnp.bfloat16)
    rotation = jnp.array(
        [[[1.0, 0.0], [0.0, -1.0]], [[0.0, 1.0], [1.0, 0.0]]], dtype=jnp.bfloat16
    )
    spread = select[:, None, :, None, None] * rotation[None, :, None, :, :]
    left_rows = jnp.einsum(
        "cwpb,cpiqr->biqrw", gathered, spread, preferred_element_type=jnp.float32
    ).astype(jnp.bfloat16).reshape(bins_here, block_rows * 2, 2 * all_windows)
    out = jnp.einsum("bik,bkj->bij", left_rows, right, preferred_element_type=jnp.float32)
    return (out / all_windows).astype(jnp.bfloat16).reshape(bins_here, block_rows, 2, total_channels)


def lines_fit(mesh):
    if dict(mesh.shape) != {"groups": mesh.shape["groups"], "chan": 16, "freq": 1}:
        return False
    devices = mesh.devices.reshape(mesh.shape["groups"], 16)
    for group in devices:
        first = getattr(group[0], "coords", None)
        if first is None:
            return False
        for position, device in enumerate(group):
            z, y, core = position // 4, (position // 2) % 2, position % 2
            where = tuple(device.coords)
            if getattr(device, "core_on_chip", None) != core:
                return False
            if where != (first[0], first[1] + y, first[2] + z):
                return False
    return True


def solution(mesh):
    return jax.shard_map(
        functools.partial(body, lines_fit(mesh)),
        mesh=mesh,
        in_specs=(
            P(("groups", "chan"), "freq", None),
            P(("groups", "chan"), "freq"),
            P("groups"),
            P("groups"),
        ),
        out_specs=P("freq", ("groups", "chan"), None, None),
        check_vma=False,
    )
```

```python
import functools
import math

import numpy as np

import jax
import jax.numpy as jnp
from jax import lax
from jax.experimental import pallas as pl
from jax.experimental.pallas import tpu as pltpu
from jax.sharding import PartitionSpec as P

WIN = 12000
NB = 512
K0 = 6
SUB = 32
LANE = 128
PADDED = 12288
TILES_PER_STEP = 48


def small_table(sample_values):
    bin_index = K0 + np.arange(NB, dtype=np.int64)
    residue = sample_values[:, None] * bin_index[None, :] % WIN
    angles = residue.astype(np.float64) * (2.0 * math.pi / WIN)
    return np.cos(angles).astype(np.float32), (-np.sin(angles)).astype(np.float32)


def constant_tables():
    high_count = PADDED // LANE
    cos_high, sin_high = small_table(np.arange(high_count, dtype=np.int64) * LANE)
    cos_low, sin_low = small_table(np.arange(LANE, dtype=np.int64))
    positions = np.arange(PADDED, dtype=np.float64)
    taper = (0.5 - 0.5 * np.cos(positions * (2.0 * math.pi / WIN))).astype(np.float32)
    groups = (np.arange(NB)[:, None] // SUB == np.arange(NB // SUB)[None, :]).astype(np.float32)
    return cos_high, sin_high, cos_low, sin_low, taper.reshape(1, PADDED), groups


def dft_kernel(
    raw_ref, code_ref, taper_ref, cos_high_ref, sin_high_ref, cos_low_ref,
    sin_low_ref, groups_ref, out_ref, total_ref, mean_ref,
):
    phase = pl.program_id(0)
    step = pl.program_id(1)
    block = TILES_PER_STEP * LANE
    lengths = code_ref[...]

    @pl.when(jnp.logical_and(phase == 0, step == 0))
    def _():
        mean_ref[...] = jnp.zeros_like(mean_ref)
        total_ref[...] = jnp.zeros_like(total_ref)

    @pl.when(phase == 0)
    def _():
        positions = step * block + lax.broadcasted_iota(jnp.int32, raw_ref.shape, 1)
        inside = positions < lengths
        kept = jnp.where(inside, raw_ref[...].astype(jnp.float32), 0.0)
        mean_ref[...] += jnp.sum(kept, axis=1, keepdims=True)

    @pl.when(phase == 1)
    def _():
        average = mean_ref[...] / lengths.astype(jnp.float32)
        cos_low = cos_low_ref[...]
        sin_low = sin_low_ref[...]
        real_total = total_ref[:, :NB]
        imag_total = total_ref[:, NB:]
        for tile in range(TILES_PER_STEP):
            row = step * TILES_PER_STEP + tile
            cos_high = cos_high_ref[pl.ds(row, 1), :]
            sin_high = sin_high_ref[pl.ds(row, 1), :]
            cos_part = (cos_high * cos_low - sin_high * sin_low).astype(jnp.bfloat16)
            sin_part = (sin_high * cos_low + cos_high * sin_low).astype(jnp.bfloat16)
            values = raw_ref[:, tile * LANE:(tile + 1) * LANE].astype(jnp.float32)
            positions = row * LANE + lax.broadcasted_iota(jnp.int32, values.shape, 1)
            taper = taper_ref[:, pl.ds(pl.multiple_of(row * LANE, LANE), LANE)]
            samples = jnp.where(
                positions < lengths, (values - average) * taper, 0.0
            ).astype(jnp.bfloat16)
            real_total = real_total + jnp.dot(samples, cos_part, preferred_element_type=jnp.float32)
            imag_total = imag_total + jnp.dot(samples, sin_part, preferred_element_type=jnp.float32)
        total_ref[:, :NB] = real_total
        total_ref[:, NB:] = imag_total

        @pl.when(step == pl.num_programs(1) - 1)
        def _():
            groups = groups_ref[...]
            power = jnp.dot(
                real_total * real_total + imag_total * imag_total,
                groups,
                precision=lax.Precision.HIGHEST,
                preferred_element_type=jnp.float32,
            ) / SUB
            factor = lax.rsqrt(power + 1e-06)
            spread = lax.dot_general(
                factor, groups, (((1,), (1,)), ((), ())),
                precision=lax.Precision.HIGHEST,
                preferred_element_type=jnp.float32,
            )
            out_ref[:, :NB] = (real_total * spread).astype(jnp.bfloat16)
            out_ref[:, NB:] = (imag_total * spread).astype(jnp.bfloat16)


def whitened_of(raw_rows, code_rows):
    row_count = raw_rows.shape[0]
    tables = [jnp.asarray(t) for t in constant_tables()]
    block = TILES_PER_STEP * LANE
    steps = PADDED // block
    full = lambda shape: pl.BlockSpec(shape, lambda p, s: (0, 0))
    return pl.pallas_call(
        dft_kernel,
        out_shape=jax.ShapeDtypeStruct((row_count, 2 * NB), jnp.bfloat16),
        grid=(2, steps),
        in_specs=[
            pl.BlockSpec((row_count, block), lambda p, s: (0, s)),
            full((row_count, 1)),
            full((1, PADDED)),
            full(tables[1].shape),
            full(tables[1].shape),
            full(tables[2].shape),
            full(tables[2].shape),
            full(tables[5].shape),
        ],
        out_specs=full((row_count, 2 * NB)),
        scratch_shapes=[
            pltpu.VMEM((row_count, 2 * NB), jnp.float32),
            pltpu.VMEM((row_count, 1), jnp.float32),
        ],
        compiler_params=pltpu.CompilerParams(dimension_semantics=("arbitrary", "arbitrary")),
        cost_estimate=pl.CostEstimate(
            flops=2 * row_count * PADDED * 2 * NB,
            transcendentals=0,
            bytes_accessed=2 * row_count * WIN * 2 + row_count * 2 * NB * 2,
        ),
    )(raw_rows, code_rows, tables[4], tables[0], tables[1], tables[2], tables[3], tables[5])


def device_index(z, y, core):
    return z * 4 + y * 2 + core


def across(valid):
    return [
        (device_index(z, y, core), device_index(z, 1 - y, core))
        for z in range(4) if valid(z) for y in range(2) for core in range(2)
    ]


def compact(own, ups, downs, z):
    line = jnp.zeros((4,) + own.shape, own.dtype)
    for hop in (3, 2, 1):
        line = lax.dynamic_update_index_in_dim(line, ups[hop - 1], jnp.maximum(z - hop, 0), 0)
    for hop in (3, 2, 1):
        line = lax.dynamic_update_index_in_dim(line, downs[hop - 1], jnp.minimum(z + hop, 3), 0)
    return lax.dynamic_update_index_in_dim(line, own, z, 0)


def line_gather(block):
    me = lax.axis_index("chan")
    z = me // 4
    y = (me // 2) % 2
    core = me % 2
    def shift(distance):
        return [
            (device_index(a, b, c), device_index(a + distance, b, c))
            for a in range(4) if 0 <= a + distance < 4 for b in range(2) for c in range(2)
        ]

    other_own = lax.ppermute(block, "chan", across(lambda a: True))
    ups = [lax.ppermute(block, "chan", shift(1)), lax.ppermute(block, "chan", shift(2))]
    downs = [lax.ppermute(block, "chan", shift(-1)), lax.ppermute(block, "chan", shift(-2))]
    ups.append(lax.ppermute(ups[1], "chan", shift(1)))
    downs.append(lax.ppermute(downs[1], "chan", shift(-1)))
    first = lax.ppermute(jnp.stack([ups[0], downs[0]]), "chan", across(lambda a: True))
    second = lax.ppermute(jnp.where(z >= 2, ups[1], downs[1]), "chan", across(lambda a: True))
    third = lax.ppermute(jnp.where(z == 3, ups[2], downs[2]), "chan", across(lambda a: a in (0, 3)))
    other = jnp.zeros((4,) + block.shape, block.dtype)
    other = lax.dynamic_update_index_in_dim(other, third, jnp.where(z == 3, 0, 3), 0)
    other = lax.dynamic_update_index_in_dim(other, second, jnp.where(z >= 2, z - 2, z + 2), 0)
    other = lax.dynamic_update_index_in_dim(other, first[0], jnp.maximum(z - 1, 0), 0)
    other = lax.dynamic_update_index_in_dim(other, first[1], jnp.minimum(z + 1, 3), 0)
    other = lax.dynamic_update_index_in_dim(other, other_own, z, 0)
    own_line = compact(block, ups, downs, z)
    pairs = [(i, i ^ 1) for i in range(16)]
    gathered = jnp.concatenate(
        [own_line, other, lax.ppermute(own_line, "chan", pairs), lax.ppermute(other, "chan", pairs)], 0
    )
    slots = jnp.arange(16, dtype=jnp.int32)
    part = slots // 4
    slot_y = jnp.where(part % 2 == 0, y, 1 - y)
    slot_core = jnp.where(part < 2, core, 1 - core)
    owner = device_index(slots % 4, slot_y, slot_core)
    return gathered.reshape((16 * block.shape[0],) + block.shape[1:]), owner


def body(use_lines, raw, lengths, quality, assignment):
    my_index = lax.axis_index("chan")
    block_rows, window_count, sample_count = raw.shape
    total_channels = assignment.shape[0]
    row_count = block_rows * window_count
    whitened = whitened_of(
        raw.reshape(row_count, sample_count), lengths.reshape(row_count, 1)
    ).reshape(block_rows, window_count, 2, NB)
    panel = lax.all_to_all(whitened, "freq", split_axis=3, concat_axis=1, tiled=True)
    all_windows = panel.shape[1]
    bins_here = panel.shape[3]
    if use_lines:
        gathered, owner = line_gather(panel)
        rows = jnp.arange(block_rows, dtype=jnp.int32)
        slot_channel = (owner[:, None] * block_rows + rows[None, :]).reshape(total_channels)
        slot_assignment = jnp.take(assignment, slot_channel)
        slot_quality = jnp.take(quality, slot_channel)
    else:
        gathered = lax.all_gather(panel, "chan", axis=0, tiled=True)
        slot_assignment = assignment
        slot_quality = quality
    good = (slot_quality != 0)[:, None]
    positions = jnp.arange(total_channels, dtype=jnp.int32)
    onehot = jnp.logical_and(slot_assignment[:, None] == positions[None, :], good).astype(jnp.bfloat16)
    right = jnp.einsum(
        "cwpb,cj->bpwj", gathered, onehot, preferred_element_type=jnp.float32
    ).astype(jnp.bfloat16).reshape(bins_here, 2 * all_windows, total_channels)
    mine = my_index * block_rows + jnp.arange(block_rows, dtype=jnp.int32)
    select = jnp.logical_and(slot_assignment[:, None] == mine[None, :], good).astype(jnp.bfloat16)
    rotation = jnp.array(
        [[[1.0, 0.0], [0.0, -1.0]], [[0.0, 1.0], [1.0, 0.0]]], dtype=jnp.bfloat16
    )
    spread = select[:, None, :, None, None] * rotation[None, :, None, :, :]
    left_rows = jnp.einsum(
        "cwpb,cpiqr->biqrw", gathered, spread, preferred_element_type=jnp.float32
    ).astype(jnp.bfloat16).reshape(bins_here, block_rows * 2, 2 * all_windows)
    out = jnp.einsum("bik,bkj->bij", left_rows, right, preferred_element_type=jnp.float32)
    return (out / all_windows).astype(jnp.bfloat16).reshape(bins_here, block_rows, 2, total_channels)


def lines_fit(mesh):
    if dict(mesh.shape) != {"groups": mesh.shape["groups"], "chan": 16, "freq": 1}:
        return False
    devices = mesh.devices.reshape(mesh.shape["groups"], 16)
    for group in devices:
        first = getattr(group[0], "coords", None)
        if first is None:
            return False
        for position, device in enumerate(group):
            z, y, core = position // 4, (position // 2) % 2, position % 2
            where = tuple(device.coords)
            if getattr(device, "core_on_chip", None) != core:
                return False
            if where != (first[0], first[1] + y, first[2] + z):
                return False
    return True


def solution(mesh):
    return jax.shard_map(
        functools.partial(body, lines_fit(mesh)),
        mesh=mesh,
        in_specs=(
            P(("groups", "chan"), "freq", None),
            P(("groups", "chan"), "freq"),
            P("groups"),
            P("groups"),
        ),
        out_specs=P("freq", ("groups", "chan"), None, None),
        check_vma=False,
    )
```

```python
import functools
import math

import numpy as np

import jax
import jax.numpy as jnp
from jax import lax
from jax.experimental import pallas as pl
from jax.experimental.pallas import tpu as pltpu
from jax.sharding import PartitionSpec as P

WIN = 12000
NB = 512
K0 = 6
SUB = 32
LANE = 128
PADDED = 12288
TILES_PER_STEP = 48


def small_table(sample_values):
    bin_index = K0 + np.arange(NB, dtype=np.int64)
    residue = sample_values[:, None] * bin_index[None, :] % WIN
    angles = residue.astype(np.float64) * (2.0 * math.pi / WIN)
    return np.cos(angles).astype(np.float32), (-np.sin(angles)).astype(np.float32)


def constant_tables():
    high_count = PADDED // LANE
    cos_high, sin_high = small_table(np.arange(high_count, dtype=np.int64) * LANE)
    cos_low, sin_low = small_table(np.arange(LANE, dtype=np.int64))
    positions = np.arange(PADDED, dtype=np.float64)
    taper = (0.5 - 0.5 * np.cos(positions * (2.0 * math.pi / WIN))).astype(np.float32)
    groups = (np.arange(NB)[:, None] // SUB == np.arange(NB // SUB)[None, :]).astype(np.float32)
    return cos_high, sin_high, cos_low, sin_low, taper.reshape(1, PADDED), groups


def dft_kernel(
    raw_ref, code_ref, taper_ref, cos_high_ref, sin_high_ref, cos_low_ref,
    sin_low_ref, groups_ref, out_ref, total_ref, mean_ref,
):
    phase = pl.program_id(0)
    step = pl.program_id(1)
    block = TILES_PER_STEP * LANE
    lengths = code_ref[...]

    @pl.when(jnp.logical_and(phase == 0, step == 0))
    def _():
        mean_ref[...] = jnp.zeros_like(mean_ref)
        total_ref[...] = jnp.zeros_like(total_ref)

    @pl.when(phase == 0)
    def _():
        first = (pl.num_programs(1) - 1 - step) * block
        positions = first + lax.broadcasted_iota(jnp.int32, raw_ref.shape, 1)
        inside = positions < lengths
        kept = jnp.where(inside, raw_ref[...].astype(jnp.float32), 0.0)
        mean_ref[...] += jnp.sum(kept, axis=1, keepdims=True)

    @pl.when(phase == 1)
    def _():
        average = mean_ref[...] / lengths.astype(jnp.float32)
        cos_low = cos_low_ref[...]
        sin_low = sin_low_ref[...]
        real_total = total_ref[:, :NB]
        imag_total = total_ref[:, NB:]
        for tile in range(TILES_PER_STEP):
            row = step * TILES_PER_STEP + tile
            cos_high = cos_high_ref[pl.ds(row, 1), :]
            sin_high = sin_high_ref[pl.ds(row, 1), :]
            cos_part = (cos_high * cos_low - sin_high * sin_low).astype(jnp.bfloat16)
            sin_part = (sin_high * cos_low + cos_high * sin_low).astype(jnp.bfloat16)
            values = raw_ref[:, tile * LANE:(tile + 1) * LANE].astype(jnp.float32)
            positions = row * LANE + lax.broadcasted_iota(jnp.int32, values.shape, 1)
            taper = taper_ref[:, pl.ds(pl.multiple_of(row * LANE, LANE), LANE)]
            samples = jnp.where(
                positions < lengths, (values - average) * taper, 0.0
            ).astype(jnp.bfloat16)
            real_total = real_total + jnp.dot(samples, cos_part, preferred_element_type=jnp.float32)
            imag_total = imag_total + jnp.dot(samples, sin_part, preferred_element_type=jnp.float32)
        total_ref[:, :NB] = real_total
        total_ref[:, NB:] = imag_total

        @pl.when(step == pl.num_programs(1) - 1)
        def _():
            groups = groups_ref[...]
            power = jnp.dot(
                real_total * real_total + imag_total * imag_total,
                groups,
                precision=lax.Precision.HIGHEST,
                preferred_element_type=jnp.float32,
            ) / SUB
            factor = lax.rsqrt(power + 1e-06)
            spread = lax.dot_general(
                factor, groups, (((1,), (1,)), ((), ())),
                precision=lax.Precision.HIGHEST,
                preferred_element_type=jnp.float32,
            )
            out_ref[:, :NB] = (real_total * spread).astype(jnp.bfloat16)
            out_ref[:, NB:] = (imag_total * spread).astype(jnp.bfloat16)


def whitened_of(raw_rows, code_rows):
    row_count = raw_rows.shape[0]
    tables = [jnp.asarray(t) for t in constant_tables()]
    block = TILES_PER_STEP * LANE
    steps = PADDED // block
    full = lambda shape: pl.BlockSpec(shape, lambda p, s: (0, 0))
    return pl.pallas_call(
        dft_kernel,
        out_shape=jax.ShapeDtypeStruct((row_count, 2 * NB), jnp.bfloat16),
        grid=(2, steps),
        in_specs=[
            pl.BlockSpec((row_count, block), lambda p, s: (0, (1 - p) * (steps - 1 - s) + p * s)),
            full((row_count, 1)),
            full((1, PADDED)),
            full(tables[1].shape),
            full(tables[1].shape),
            full(tables[2].shape),
            full(tables[2].shape),
            full(tables[5].shape),
        ],
        out_specs=full((row_count, 2 * NB)),
        scratch_shapes=[
            pltpu.VMEM((row_count, 2 * NB), jnp.float32),
            pltpu.VMEM((row_count, 1), jnp.float32),
        ],
        compiler_params=pltpu.CompilerParams(dimension_semantics=("arbitrary", "arbitrary")),
        cost_estimate=pl.CostEstimate(
            flops=2 * row_count * PADDED * 2 * NB,
            transcendentals=0,
            bytes_accessed=2 * row_count * WIN * 2 + row_count * 2 * NB * 2,
        ),
    )(raw_rows, code_rows, tables[4], tables[0], tables[1], tables[2], tables[3], tables[5])


def device_index(z, y, core):
    return z * 4 + y * 2 + core


def across(valid):
    return [
        (device_index(z, y, core), device_index(z, 1 - y, core))
        for z in range(4) if valid(z) for y in range(2) for core in range(2)
    ]


def compact(own, ups, downs, z):
    line = jnp.zeros((4,) + own.shape, own.dtype)
    for hop in (3, 2, 1):
        line = lax.dynamic_update_index_in_dim(line, ups[hop - 1], jnp.maximum(z - hop, 0), 0)
    for hop in (3, 2, 1):
        line = lax.dynamic_update_index_in_dim(line, downs[hop - 1], jnp.minimum(z + hop, 3), 0)
    return lax.dynamic_update_index_in_dim(line, own, z, 0)


def line_gather(block):
    me = lax.axis_index("chan")
    z = me // 4
    y = (me // 2) % 2
    core = me % 2
    def shift(distance):
        return [
            (device_index(a, b, c), device_index(a + distance, b, c))
            for a in range(4) if 0 <= a + distance < 4 for b in range(2) for c in range(2)
        ]

    other_own = lax.ppermute(block, "chan", across(lambda a: True))
    ups = [lax.ppermute(block, "chan", shift(1)), lax.ppermute(block, "chan", shift(2))]
    downs = [lax.ppermute(block, "chan", shift(-1)), lax.ppermute(block, "chan", shift(-2))]
    ups.append(lax.ppermute(ups[1], "chan", shift(1)))
    downs.append(lax.ppermute(downs[1], "chan", shift(-1)))
    first = lax.ppermute(jnp.stack([ups[0], downs[0]]), "chan", across(lambda a: True))
    second = lax.ppermute(jnp.where(z >= 2, ups[1], downs[1]), "chan", across(lambda a: True))
    third = lax.ppermute(jnp.where(z == 3, ups[2], downs[2]), "chan", across(lambda a: a in (0, 3)))
    other = jnp.zeros((4,) + block.shape, block.dtype)
    other = lax.dynamic_update_index_in_dim(other, third, jnp.where(z == 3, 0, 3), 0)
    other = lax.dynamic_update_index_in_dim(other, second, jnp.where(z >= 2, z - 2, z + 2), 0)
    other = lax.dynamic_update_index_in_dim(other, first[0], jnp.maximum(z - 1, 0), 0)
    other = lax.dynamic_update_index_in_dim(other, first[1], jnp.minimum(z + 1, 3), 0)
    other = lax.dynamic_update_index_in_dim(other, other_own, z, 0)
    both = jnp.concatenate([compact(block, ups, downs, z), other], 0)
    sibling = lax.ppermute(both, "chan", [(i, i ^ 1) for i in range(16)])
    gathered = jnp.concatenate([both, sibling], 0)
    slots = jnp.arange(16, dtype=jnp.int32)
    part = slots // 4
    slot_y = jnp.where(part % 2 == 0, y, 1 - y)
    slot_core = jnp.where(part < 2, core, 1 - core)
    owner = device_index(slots % 4, slot_y, slot_core)
    return gathered.reshape((16 * block.shape[0],) + block.shape[1:]), owner


def body(use_lines, raw, lengths, quality, assignment):
    my_index = lax.axis_index("chan")
    block_rows, window_count, sample_count = raw.shape
    total_channels = assignment.shape[0]
    row_count = block_rows * window_count
    whitened = whitened_of(
        raw.reshape(row_count, sample_count), lengths.reshape(row_count, 1)
    ).reshape(block_rows, window_count, 2, NB)
    panel = lax.all_to_all(whitened, "freq", split_axis=3, concat_axis=1, tiled=True)
    all_windows = panel.shape[1]
    bins_here = panel.shape[3]
    if use_lines:
        gathered, owner = line_gather(panel)
        rows = jnp.arange(block_rows, dtype=jnp.int32)
        slot_channel = (owner[:, None] * block_rows + rows[None, :]).reshape(total_channels)
        slot_assignment = jnp.take(assignment, slot_channel)
        slot_quality = jnp.take(quality, slot_channel)
    else:
        gathered = lax.all_gather(panel, "chan", axis=0, tiled=True)
        slot_assignment = assignment
        slot_quality = quality
    good = (slot_quality != 0)[:, None]
    positions = jnp.arange(total_channels, dtype=jnp.int32)
    onehot = jnp.logical_and(slot_assignment[:, None] == positions[None, :], good).astype(jnp.bfloat16)
    right = jnp.einsum(
        "cwpb,cj->bpwj", gathered, onehot, preferred_element_type=jnp.float32
    ).astype(jnp.bfloat16).reshape(bins_here, 2 * all_windows, total_channels)
    mine = my_index * block_rows + jnp.arange(block_rows, dtype=jnp.int32)
    select = jnp.logical_and(slot_assignment[:, None] == mine[None, :], good).astype(jnp.bfloat16)
    rotation = jnp.array(
        [[[1.0, 0.0], [0.0, -1.0]], [[0.0, 1.0], [1.0, 0.0]]], dtype=jnp.bfloat16
    )
    spread = select[:, None, :, None, None] * rotation[None, :, None, :, :]
    left_rows = jnp.einsum(
        "cwpb,cpiqr->biqrw", gathered, spread, preferred_element_type=jnp.float32
    ).astype(jnp.bfloat16).reshape(bins_here, block_rows * 2, 2 * all_windows)
    out = jnp.einsum("bik,bkj->bij", left_rows, right, preferred_element_type=jnp.float32)
    return (out / all_windows).astype(jnp.bfloat16).reshape(bins_here, block_rows, 2, total_channels)


def lines_fit(mesh):
    if dict(mesh.shape) != {"groups": mesh.shape["groups"], "chan": 16, "freq": 1}:
        return False
    devices = mesh.devices.reshape(mesh.shape["groups"], 16)
    for group in devices:
        first = getattr(group[0], "coords", None)
        if first is None:
            return False
        for position, device in enumerate(group):
            z, y, core = position // 4, (position // 2) % 2, position % 2
            where = tuple(device.coords)
            if getattr(device, "core_on_chip", None) != core:
                return False
            if where != (first[0], first[1] + y, first[2] + z):
                return False
    return True


def solution(mesh):
    return jax.shard_map(
        functools.partial(body, lines_fit(mesh)),
        mesh=mesh,
        in_specs=(
            P(("groups", "chan"), "freq", None),
            P(("groups", "chan"), "freq"),
            P("groups"),
            P("groups"),
        ),
        out_specs=P("freq", ("groups", "chan"), None, None),
        check_vma=False,
    )
```
